128 devices in a mesh: seq: 128 (over y, x, z, core).
Axes of the slice: x: 4, y: 4, z: 4, core: 2. Of those that a mesh axis runs over, the one named last changes fastest.
Arguments:
- queries: bfloat16 [16384, 8192], P('seq'), may hold values from -5.1 to 5.1
- keys: bfloat16 [16384, 1024], P('seq'), may hold values from -5.1 to 5.1
- values: bfloat16 [16384, 1024], P('seq'), may hold values from -6 to 6
- lengths: int32 [32], replicated, may hold values from 1 to 8, 128 in all
- class_weight: bfloat16 [8192, 16], replicated, may hold values from -0.25 to 0.25
Outputs:
- attended: bfloat16 [16384, 8192], P('seq')
- doc_logits: float32 [128, 16], P('seq')
The draws below stay inside these ranges and needn't reach their ends.
Inputs may be any that keep to these rules, and one draw needn't show every extreme that they name: `lengths`: lengths are counted in blocks of 128 tokens; they sum to 128 and the longest is exactly 8 blocks.
All inputs are finite; a program needn't handle non-finite values.
Results may differ from the reference program's by a relative error of at most 0.0046.
Values may be sent and summed in bfloat16 or wider, within the bound.
No kernel may reach another device: no remote copies, remote signals or barrier semaphores. Data moves between devices by JAX's collectives and lax.ppermute only.
A program may use at most 192 MiB of HBM per device.

```python
import math
import jax
import jax.numpy as jnp
import numpy as np
from jax import lax

H = 64
KVH = 8
DH = 128
BLK = 128
MAXB = 8
NCLASS = 16
TOK_DEV = 128
REACH = 7
TOKENS = 16384
NBLK = 128
NDOC = 32
N_SEQ = 128


def banded(array):
    width = array.shape[1]
    stripe = TOK_DEV // N_SEQ
    return array.reshape(N_SEQ, N_SEQ, stripe, width).transpose(1, 0, 2, 3).reshape(TOKENS, width)


def draw_queries(key, part):
    branch_key = jax.random.fold_in(key, 21)
    result = jnp.clip(jax.random.normal(branch_key, (TOKENS, H, DH)), -5.0, 5.0)
    return banded(result.reshape(TOKENS, H * DH)).astype(jnp.bfloat16)


def draw_keys(key, part):
    branch_key = jax.random.fold_in(key, 31)
    result = jnp.clip(jax.random.normal(branch_key, (TOKENS, KVH, DH)), -5.0, 5.0)
    return banded(result.reshape(TOKENS, KVH * DH)).astype(jnp.bfloat16)


def block_scale(rng, extent, shards, least, high):
    level = 1.0
    for dim, shards_of in shards:
        steps = jax.random.uniform(jax.random.fold_in(jax.random.fold_in(rng, 6), dim), (shards_of,), jnp.float32, least / len(shards), high / len(shards))
        level = level * jnp.repeat(jnp.exp(steps), extent[dim] // shards_of).reshape((-1,) + (1,) * (len(extent) - 1 - dim))
    return level


def split_up(amount, total, reach, lean):
    loads = [(1 << 20) // math.isqrt(grade ** lean) + 1 for grade in range(2, amount + 1)]
    spare, counts = total - reach - (amount - 1), [1] * (amount - 1)
    while spare > 0:
        movable = [i for i in range(amount - 1) if counts[i] < reach]
        mass, left = sum([loads[i] for i in movable]), spare
        for i in movable:
            more = min(reach - counts[i], max(1, left * loads[i] // mass), spare)
            counts[i] = counts[i] + more
            spare = spare - more
    return np.array([reach] + counts)


def ragged(key, count, total, reach, skew):
    if count == 2:
        one = jax.random.randint(key, (), max(1, total - reach), min(reach, total - 1) + 1)
        return jnp.stack([one, total - one])
    tallies = jnp.asarray(split_up(count, total, reach, skew), jnp.int32)
    pairs = (count - 1) // 2
    source_of, taker = tallies[1:1 + 2 * pairs:2], tallies[2:2 + 2 * pairs:2]
    room = jnp.minimum(source_of - 1, reach - taker)
    passed = jax.random.randint(jax.random.fold_in(key, 1), (pairs,), 0, 1 << 20) % (room + 1)
    tallies = tallies.at[1:1 + 2 * pairs:2].set(source_of - passed).at[2:2 + 2 * pairs:2].set(taker + passed)
    return tallies[jax.random.permutation(jax.random.fold_in(key, 2), count)]


def scatter_about(stream_key, extent, scale, most, shards=(), kind=jnp.bfloat16):
    values = jax.random.normal(stream_key, extent, jnp.float32) * scale
    if len(shards) > 0:
        values = block_scale(stream_key, extent, shards, -0.22, 0.18) * values
    return jnp.clip(values, min=-most, max=most).astype(kind)


def setup_inputs(seed: int = 0) -> dict:
    key_of = jax.random.split(jax.random.key(seed), 6)
    return {
        "queries": draw_queries(jax.random.fold_in(key_of[5], 71), 0),
        "keys": draw_keys(jax.random.fold_in(key_of[5], 71), 0),
        "values": scatter_about(key_of[2], (TOKENS, KVH * DH), 1.0, 6.0, ((0, 128),)),
        "lengths": ragged(key_of[3], NDOC, NBLK, MAXB, 2).astype(jnp.int32),
        "class_weight": scatter_about(key_of[4], (H * DH, NCLASS), (H * DH // 16) ** -0.5, 0.25),
    }


NEGATIVE = -1e30


def token_order(array):
    width = array.shape[1]
    stripe = TOK_DEV // N_SEQ
    return array.reshape(N_SEQ, N_SEQ, stripe, width).transpose(1, 0, 2, 3).reshape(TOKENS, width)


def block_docs(lengths, block_count):
    doc_ends = jnp.cumsum(lengths, dtype=jnp.int32)
    doc_firsts = doc_ends - lengths
    blocks = jnp.arange(block_count, dtype=jnp.int32)
    owner_doc = jnp.sum((doc_ends[None, :] <= blocks[:, None]).astype(jnp.int32), axis=1).astype(jnp.int32)
    matches = owner_doc[:, None] == jnp.arange(lengths.shape[0], dtype=jnp.int32)[None, :]
    first_block = jnp.sum(jnp.where(matches, doc_firsts[None, :], 0), axis=1).astype(jnp.int32)
    return owner_doc, first_block


def empty_terms(query_tiles):
    heads_kv = query_tiles.shape[1]
    group = query_tiles.shape[2]
    row_count = query_tiles.shape[0]
    width = query_tiles.shape[3]
    return (jnp.full((heads_kv, group, row_count), NEGATIVE, jnp.float32),
            jnp.zeros((heads_kv, group, row_count), jnp.float32),
            jnp.zeros((heads_kv, group, row_count, width), jnp.float32))


def tile_terms(query_tiles, key_part, value_part, linked):
    factor = query_tiles.shape[-1] ** -0.5
    scores = jnp.einsum("qkgd,skd->kgqs", query_tiles.astype(jnp.float32), key_part.astype(jnp.float32)) * factor
    scores = jnp.where(linked[None, None], scores, NEGATIVE)
    row_max = jnp.max(scores, axis=-1, keepdims=True)
    weights = jnp.where(linked[None, None], jnp.exp(scores - row_max), 0.0)
    weight_sum = jnp.sum(weights, axis=-1)
    rounded = weights.astype(jnp.bfloat16)
    partial_value = jnp.einsum("kgqs,skd->kgqd", rounded.astype(jnp.float32), value_part.astype(jnp.float32))
    return row_max[..., 0], weight_sum, partial_value


def absorb(running, tile_parts):
    old_max, old_sum, old_out = running
    tile_max, tile_sum, tile_out = tile_parts
    new_max = jnp.maximum(old_max, tile_max)
    keep_old = jnp.exp(old_max - new_max)
    keep_new = jnp.exp(tile_max - new_max)
    return (new_max, old_sum * keep_old + tile_sum * keep_new,
            old_out * keep_old[..., None] + tile_out * keep_new[..., None])


def reference(queries, keys, values, lengths, class_weight):
    queries = token_order(queries)
    keys = token_order(keys)
    values = token_order(values)
    owner_doc, first_block = block_docs(lengths, NBLK)
    token_docs = jnp.repeat(owner_doc, BLK)
    group = H // KVH
    query_all = queries.reshape(N_SEQ, TOK_DEV, KVH, group, DH)
    key_all = keys.reshape(N_SEQ, TOK_DEV, KVH, DH)
    value_all = values.reshape(N_SEQ, TOK_DEV, KVH, DH)
    doc_all = token_docs.reshape(N_SEQ, TOK_DEV)

    def one_shard(shard):
        query_tiles = lax.dynamic_index_in_dim(query_all, shard, 0, keepdims=False)
        own_docs = lax.dynamic_index_in_dim(doc_all, shard, 0, keepdims=False)
        running = empty_terms(query_tiles)
        for offset in range(-REACH, REACH + 1):
            source = shard + offset
            inside = (source >= 0) & (source < N_SEQ)
            clipped = jnp.clip(source, 0, N_SEQ - 1).astype(jnp.int32)
            key_part = lax.dynamic_index_in_dim(key_all, clipped, 0, keepdims=False)
            value_part = lax.dynamic_index_in_dim(value_all, clipped, 0, keepdims=False)
            source_docs = lax.dynamic_index_in_dim(doc_all, clipped, 0, keepdims=False)
            linked = (own_docs[:, None] == source_docs[None, :]) & inside
            tile_parts = lax.cond(jnp.any(linked),
                                  lambda: tile_terms(query_tiles, key_part, value_part, linked),
                                  lambda: empty_terms(query_tiles))
            running = absorb(running, tile_parts)
        row_max, weight_sum, summed = running
        normed = summed / weight_sum[..., None]
        return normed.transpose(2, 0, 1, 3).reshape(TOK_DEV, H * DH).astype(jnp.bfloat16)

    attended = lax.map(one_shard, jnp.arange(N_SEQ, dtype=jnp.int32)).reshape(TOKENS, H * DH)
    firsts = attended.reshape(NBLK, BLK, H * DH)[:, 0, :]
    chosen_rows = firsts[first_block]
    doc_logits = jnp.dot(chosen_rows, class_weight, preferred_element_type=jnp.float32)
    return attended, doc_logits
```

```python
import jax
import jax.numpy as jnp
from jax import lax
from jax.sharding import PartitionSpec as P

DH = 128
BLK = 128
MAXB = 8


def shifted(block, axis, distance):
    count = lax.axis_size(axis)
    if distance > 0:
        route = [(i - distance, i) for i in range(distance, count)]
    else:
        route = [(i - distance, i) for i in range(0, count + distance)]
    return lax.ppermute(block, axis, route)


def block_docs(lengths, block_count):
    doc_ends = jnp.cumsum(lengths, dtype=jnp.int32)
    doc_firsts = doc_ends - lengths
    blocks = jnp.arange(block_count, dtype=jnp.int32)
    owner_doc = jnp.sum((doc_ends[None, :] <= blocks[:, None]).astype(jnp.int32), axis=1)
    matches = owner_doc[:, None] == jnp.arange(lengths.shape[0], dtype=jnp.int32)[None, :]
    first_block = jnp.sum(jnp.where(matches, doc_firsts[None, :], 0), axis=1)
    return (owner_doc, first_block)


def tile_terms(query_tiles, key_part, value_part):
    factor = query_tiles.shape[-1] ** (-0.5)
    scores = (
        jnp.einsum("qkgd,skd->kgqs", query_tiles, key_part, preferred_element_type=jnp.float32)
        * factor
    )
    row_max = jnp.max(scores, axis=-1, keepdims=True)
    weights = jnp.exp(scores - row_max)
    weight_sum = jnp.sum(weights, axis=-1)
    rounded = weights.astype(jnp.bfloat16)
    partial_value = jnp.einsum(
        "kgqs,skd->kgqd", rounded, value_part, preferred_element_type=jnp.float32
    )
    return (row_max[..., 0], weight_sum, partial_value)


def absorb(running, tile_parts):
    old_max, old_sum, old_out = running
    tile_max, tile_sum, tile_out = tile_parts
    new_max = jnp.maximum(old_max, tile_max)
    keep_old = jnp.exp(old_max - new_max)
    keep_new = jnp.exp(tile_max - new_max)
    return (
        new_max,
        old_sum * keep_old + tile_sum * keep_new,
        old_out * keep_old[..., None] + tile_out * keep_new[..., None],
    )


def shards(queries, keys, values, lengths, class_weight):
    devices = lax.axis_size("seq")
    myself = lax.axis_index("seq")
    row_count = queries.shape[0]
    run_rows = row_count // devices
    width_q = queries.shape[1]
    width_k = keys.shape[1]
    arrived_q = lax.all_to_all(
        queries.reshape(devices, run_rows, width_q), "seq", split_axis=0, concat_axis=0, tiled=True
    )
    arrived_kv = lax.all_to_all(
        jnp.concatenate([keys, values], axis=1).reshape(devices, run_rows, 2 * width_k),
        "seq",
        split_axis=0,
        concat_axis=0,
        tiled=True,
    )
    queries = arrived_q.reshape(row_count, width_q)
    kv = arrived_kv.reshape(row_count, 2 * width_k)
    heads_kv = width_k // DH
    group = width_q // (heads_kv * DH)
    query_tiles = queries.reshape(row_count, heads_kv, group, DH)
    owner_doc, first_block = block_docs(lengths, devices)
    my_doc = owner_doc[myself]
    reach = MAXB - 1

    def split(piece):
        return (
            piece[:, :width_k].reshape(row_count, heads_kv, DH),
            piece[:, width_k:].reshape(row_count, heads_kv, DH),
        )

    own_k, own_v = split(kv)
    running = tile_terms(query_tiles, own_k, own_v)
    right = kv
    left = kv
    for hop in range(1, reach + 1):
        right = shifted(right, "seq", 1)
        left = shifted(left, "seq", -1)
        for piece, source in ((right, myself - hop), (left, myself + hop)):
            inside = (source >= 0) & (source < devices)
            clipped = jnp.clip(source, 0, devices - 1)
            linked = inside & (owner_doc[clipped] == my_doc)
            key_part, value_part = split(piece)
            running = lax.cond(
                linked,
                lambda r, k, v: absorb(r, tile_terms(query_tiles, k, v)),
                lambda r, k, v: r,
                running,
                key_part,
                value_part,
            )
    row_max, weight_sum, summed = running
    normed = summed / weight_sum[..., None]
    attended = normed.transpose(2, 0, 1, 3).reshape(row_count, width_q).astype(jnp.bfloat16)
    own_logits = jnp.dot(attended[0:1], class_weight, preferred_element_type=jnp.float32)
    candidates = [own_logits] + [shifted(own_logits, "seq", d) for d in range(1, reach + 1)]
    distance = jnp.clip(myself - first_block[myself], 0, reach)
    doc_logits = lax.dynamic_index_in_dim(jnp.stack(candidates), distance, 0, False)
    return (attended, doc_logits)


def solution(mesh):
    return jax.shard_map(
        shards,
        mesh=mesh,
        in_specs=(P("seq", None), P("seq", None), P("seq", None), P(), P()),
        out_specs=(P("seq", None), P("seq", None)),
        check_vma=False,
    )
```

```python
import jax
import jax.numpy as jnp
from jax import lax
from jax.sharding import PartitionSpec as P
from jax.experimental import pallas as pl
from jax.experimental.pallas import tpu as pltpu

DH = 128
BLK = 128
MAXB = 8


def shifted(block, axis, distance):
    count = lax.axis_size(axis)
    if distance > 0:
        route = [(i - distance, i) for i in range(distance, count)]
    else:
        route = [(i - distance, i) for i in range(0, count + distance)]
    return lax.ppermute(block, axis, route)


def block_docs(lengths, block_count):
    doc_ends = jnp.cumsum(lengths, dtype=jnp.int32)
    doc_firsts = doc_ends - lengths
    blocks = jnp.arange(block_count, dtype=jnp.int32)
    owner_doc = jnp.sum((doc_ends[None, :] <= blocks[:, None]).astype(jnp.int32), axis=1)
    matches = owner_doc[:, None] == jnp.arange(lengths.shape[0], dtype=jnp.int32)[None, :]
    first_block = jnp.sum(jnp.where(matches, doc_firsts[None, :], 0), axis=1)
    return (owner_doc, first_block)


def attention_kernel(flags_ref, q_ref, *refs):
    kv_refs = refs[:-1]
    out_ref = refs[-1]
    width_k = kv_refs[0].shape[1] // 2
    heads = q_ref.shape[1] // DH
    group = heads // (width_k // DH)
    factor = DH ** (-0.5)

    def one_head(j, carry):
        qcol = pl.multiple_of(j * DH, DH)
        kcol = pl.multiple_of((j // group) * DH, DH)
        vcol = pl.multiple_of(width_k + (j // group) * DH, DH)
        q = q_ref[:, pl.ds(qcol, DH)]

        def tile(kv_ref):
            k = kv_ref[:, pl.ds(kcol, DH)]
            v = kv_ref[:, pl.ds(vcol, DH)]
            s = (
                lax.dot_general(q, k, (((1,), (1,)), ((), ())), preferred_element_type=jnp.float32)
                * factor
            )
            m = jnp.max(s, axis=1, keepdims=True)
            p = jnp.exp(s - m)
            l = jnp.sum(p, axis=1, keepdims=True)
            o = jnp.dot(p.astype(jnp.bfloat16), v, preferred_element_type=jnp.float32)
            return m, l, o

        state = tile(kv_refs[0])
        for t in range(1, len(kv_refs)):

            def take(state, kv_ref=kv_refs[t]):
                m0, l0, o0 = state
                m1, l1, o1 = tile(kv_ref)
                mn = jnp.maximum(m0, m1)
                a = jnp.exp(m0 - mn)
                b = jnp.exp(m1 - mn)
                return mn, l0 * a + l1 * b, o0 * a + o1 * b

            state = lax.cond(flags_ref[t] > 0, take, lambda s: s, state)
        m, l, o = state
        out_ref[:, pl.ds(qcol, DH)] = (o / l).astype(out_ref.dtype)
        return carry

    lax.fori_loop(0, heads, one_head, 0)


def attend(flags, queries, pieces):
    return pl.pallas_call(
        attention_kernel,
        out_shape=jax.ShapeDtypeStruct(queries.shape, jnp.bfloat16),
        in_specs=[pl.BlockSpec(memory_space=pltpu.SMEM)]
        + [pl.BlockSpec(memory_space=pltpu.VMEM)] * (1 + len(pieces)),
        out_specs=pl.BlockSpec(memory_space=pltpu.VMEM),
        compiler_params=pltpu.CompilerParams(vmem_limit_bytes=48 * 1024 * 1024),
    )(flags, queries, *pieces)


def shards(queries, keys, values, lengths, class_weight):
    devices = lax.axis_size("seq")
    myself = lax.axis_index("seq")
    row_count = queries.shape[0]
    run_rows = row_count // devices
    width_q = queries.shape[1]
    width_k = keys.shape[1]
    arrived_q = lax.all_to_all(
        queries.reshape(devices, run_rows, width_q), "seq", split_axis=0, concat_axis=0, tiled=True
    )
    arrived_kv = lax.all_to_all(
        jnp.concatenate([keys, values], axis=1).reshape(devices, run_rows, 2 * width_k),
        "seq",
        split_axis=0,
        concat_axis=0,
        tiled=True,
    )
    queries = arrived_q.reshape(row_count, width_q)
    kv = arrived_kv.reshape(row_count, 2 * width_k)
    owner_doc, first_block = block_docs(lengths, devices)
    my_doc = owner_doc[myself]
    reach = MAXB - 1
    pieces = [kv]
    flags = [jnp.ones((), jnp.int32)]
    right = kv
    left = kv
    for hop in range(1, reach + 1):
        right = shifted(right, "seq", 1)
        left = shifted(left, "seq", -1)
        for piece, source in ((right, myself - hop), (left, myself + hop)):
            inside = (source >= 0) & (source < devices)
            clipped = jnp.clip(source, 0, devices - 1)
            pieces.append(piece)
            flags.append((inside & (owner_doc[clipped] == my_doc)).astype(jnp.int32))
    attended = attend(jnp.stack(flags), queries, pieces)
    own_logits = jnp.dot(attended[0:1], class_weight, preferred_element_type=jnp.float32)
    candidates = [own_logits] + [shifted(own_logits, "seq", d) for d in range(1, reach + 1)]
    distance = jnp.clip(myself - first_block[myself], 0, reach)
    doc_logits = lax.dynamic_index_in_dim(jnp.stack(candidates), distance, 0, False)
    return (attended, doc_logits)


def solution(mesh):
    return jax.shard_map(
        shards,
        mesh=mesh,
        in_specs=(P("seq", None), P("seq", None), P("seq", None), P(), P()),
        out_specs=(P("seq", None), P("seq", None)),
        check_vma=False,
    )
```

```python
import jax
import jax.numpy as jnp
from jax import lax
from jax.sharding import PartitionSpec as P
from jax.experimental import pallas as pl
from jax.experimental.pallas import tpu as pltpu

DH = 128
BLK = 128
MAXB = 8


def shifted(block, axis, distance):
    count = lax.axis_size(axis)
    if distance > 0:
        route = [(i - distance, i) for i in range(distance, count)]
    else:
        route = [(i - distance, i) for i in range(0, count + distance)]
    return lax.ppermute(block, axis, route)


def block_docs(lengths, block_count):
    doc_ends = jnp.cumsum(lengths, dtype=jnp.int32)
    doc_firsts = doc_ends - lengths
    blocks = jnp.arange(block_count, dtype=jnp.int32)
    owner_doc = jnp.sum((doc_ends[None, :] <= blocks[:, None]).astype(jnp.int32), axis=1)
    matches = owner_doc[:, None] == jnp.arange(lengths.shape[0], dtype=jnp.int32)[None, :]
    first_block = jnp.sum(jnp.where(matches, doc_firsts[None, :], 0), axis=1)
    return (owner_doc, first_block)


def attention_kernel(flags_ref, q_ref, *refs):
    tiles = len(refs) - 5
    kv_refs = refs[:tiles]
    out_ref, qs_ref, m_ref, l_ref, acc_ref = refs[tiles:]
    heads_kv = qs_ref.shape[0]
    rows = q_ref.shape[0]
    group = qs_ref.shape[1] // rows
    width_k = heads_kv * DH
    factor = DH ** (-0.5)
    for h in range(heads_kv):
        for g in range(group):
            qs_ref[h, g * rows : (g + 1) * rows, :] = q_ref[:, (h * group + g) * DH : (h * group + g + 1) * DH]

    def tile_step(kv_ref, first):
        def one_head(h, carry):
            kcol = pl.multiple_of(h * DH, DH)
            vcol = pl.multiple_of(width_k + h * DH, DH)
            k = kv_ref[:, pl.ds(kcol, DH)]
            v = kv_ref[:, pl.ds(vcol, DH)]
            s = (
                lax.dot_general(
                    qs_ref[h], k, (((1,), (1,)), ((), ())), preferred_element_type=jnp.float32
                )
                * factor
            )
            m1 = jnp.max(s, axis=1, keepdims=True)
            p = jnp.exp(s - m1)
            l1 = jnp.sum(p, axis=1, keepdims=True)
            o1 = jnp.dot(p.astype(jnp.bfloat16), v, preferred_element_type=jnp.float32)
            if first:
                m_ref[h] = m1
                l_ref[h] = l1
                acc_ref[h] = o1
            else:
                m0 = m_ref[h]
                mn = jnp.maximum(m0, m1)
                a = jnp.exp(m0 - mn)
                b = jnp.exp(m1 - mn)
                m_ref[h] = mn
                l_ref[h] = l_ref[h] * a + l1 * b
                acc_ref[h] = acc_ref[h] * a + o1 * b
            return carry

        lax.fori_loop(0, heads_kv, one_head, 0)

    tile_step(kv_refs[0], True)
    for t in range(1, tiles):

        @pl.when(flags_ref[t] > 0)
        def _(kv_ref=kv_refs[t]):
            tile_step(kv_ref, False)

    for h in range(heads_kv):
        normed = acc_ref[h] / l_ref[h]
        for g in range(group):
            out_ref[:, (h * group + g) * DH : (h * group + g + 1) * DH] = normed[
                g * rows : (g + 1) * rows
            ].astype(out_ref.dtype)


def attend(flags, queries, pieces):
    rows = queries.shape[0]
    heads_kv = pieces[0].shape[1] // (2 * DH)
    group = queries.shape[1] // (heads_kv * DH)
    return pl.pallas_call(
        attention_kernel,
        out_shape=jax.ShapeDtypeStruct(queries.shape, jnp.bfloat16),
        in_specs=[pl.BlockSpec(memory_space=pltpu.SMEM)]
        + [pl.BlockSpec(memory_space=pltpu.VMEM)] * (1 + len(pieces)),
        out_specs=pl.BlockSpec(memory_space=pltpu.VMEM),
        scratch_shapes=[
            pltpu.VMEM((heads_kv, group * rows, DH), jnp.bfloat16),
            pltpu.VMEM((heads_kv, group * rows, 1), jnp.float32),
            pltpu.VMEM((heads_kv, group * rows, 1), jnp.float32),
            pltpu.VMEM((heads_kv, group * rows, DH), jnp.float32),
        ],
        compiler_params=pltpu.CompilerParams(vmem_limit_bytes=56 * 1024 * 1024),
    )(flags, queries, *pieces)


def shards(queries, keys, values, lengths, class_weight):
    devices = lax.axis_size("seq")
    myself = lax.axis_index("seq")
    row_count = queries.shape[0]
    run_rows = row_count // devices
    width_q = queries.shape[1]
    width_k = keys.shape[1]
    arrived_q = lax.all_to_all(
        queries.reshape(devices, run_rows, width_q), "seq", split_axis=0, concat_axis=0, tiled=True
    )
    arrived_kv = lax.all_to_all(
        jnp.concatenate([keys, values], axis=1).reshape(devices, run_rows, 2 * width_k),
        "seq",
        split_axis=0,
        concat_axis=0,
        tiled=True,
    )
    queries = arrived_q.reshape(row_count, width_q)
    kv = arrived_kv.reshape(row_count, 2 * width_k)
    owner_doc, first_block = block_docs(lengths, devices)
    my_doc = owner_doc[myself]
    reach = MAXB - 1
    pieces = [kv]
    flags = [jnp.ones((), jnp.int32)]
    right = kv
    left = kv
    for hop in range(1, reach + 1):
        right = shifted(right, "seq", 1)
        left = shifted(left, "seq", -1)
        for piece, source in ((right, myself - hop), (left, myself + hop)):
            inside = (source >= 0) & (source < devices)
            clipped = jnp.clip(source, 0, devices - 1)
            pieces.append(piece)
            flags.append((inside & (owner_doc[clipped] == my_doc)).astype(jnp.int32))
    attended = attend(jnp.stack(flags), queries, pieces)
    own_logits = jnp.dot(attended[0:1], class_weight, preferred_element_type=jnp.float32)
    candidates = [own_logits] + [shifted(own_logits, "seq", d) for d in range(1, reach + 1)]
    distance = jnp.clip(myself - first_block[myself], 0, reach)
    doc_logits = lax.dynamic_index_in_dim(jnp.stack(candidates), distance, 0, False)
    return (attended, doc_logits)


def solution(mesh):
    return jax.shard_map(
        shards,
        mesh=mesh,
        in_specs=(P("seq", None), P("seq", None), P("seq", None), P(), P()),
        out_specs=(P("seq", None), P("seq", None)),
        check_vma=False,
    )
```

```python
import jax
import jax.numpy as jnp
from jax import lax
from jax.sharding import PartitionSpec as P
from jax.experimental import pallas as pl
from jax.experimental.pallas import tpu as pltpu

DH = 128
BLK = 128
MAXB = 8


def shifted(block, axis, distance):
    count = lax.axis_size(axis)
    if distance > 0:
        route = [(i - distance, i) for i in range(distance, count)]
    else:
        route = [(i - distance, i) for i in range(0, count + distance)]
    return lax.ppermute(block, axis, route)


def block_docs(lengths, block_count):
    doc_ends = jnp.cumsum(lengths, dtype=jnp.int32)
    doc_firsts = doc_ends - lengths
    blocks = jnp.arange(block_count, dtype=jnp.int32)
    owner_doc = jnp.sum((doc_ends[None, :] <= blocks[:, None]).astype(jnp.int32), axis=1)
    matches = owner_doc[:, None] == jnp.arange(lengths.shape[0], dtype=jnp.int32)[None, :]
    first_block = jnp.sum(jnp.where(matches, doc_firsts[None, :], 0), axis=1)
    return (owner_doc, first_block)


def attention_kernel(flags_ref, q_ref, *refs):
    tiles = len(refs) - 5
    kv_refs = refs[:tiles]
    out_ref, qt_ref, m_ref, l_ref, acc_ref = refs[tiles:]
    heads = q_ref.shape[1] // DH
    width_k = kv_refs[0].shape[1] // 2
    heads_kv = width_k // DH
    group = heads // heads_kv
    factor = DH ** (-0.5)

    def prep(j, carry):
        col = pl.multiple_of(j * DH, DH)
        qt_ref[j] = q_ref[:, pl.ds(col, DH)].astype(jnp.float32).T.astype(jnp.bfloat16)
        return carry

    lax.fori_loop(0, heads, prep, 0)

    def tile_step(kv_ref, first):
        def one_head(h, carry):
            kcol = pl.multiple_of(h * DH, DH)
            vcol = pl.multiple_of(width_k + h * DH, DH)
            k = kv_ref[:, pl.ds(kcol, DH)]
            vt = kv_ref[:, pl.ds(vcol, DH)].astype(jnp.float32).T.astype(jnp.bfloat16)
            for g in range(group):
                j = h * group + g
                st = jnp.dot(k, qt_ref[j], preferred_element_type=jnp.float32) * factor
                m1 = jnp.max(st, axis=0, keepdims=True)
                p = jnp.exp(st - m1)
                l1 = jnp.sum(p, axis=0, keepdims=True)
                ot = jnp.dot(vt, p.astype(jnp.bfloat16), preferred_element_type=jnp.float32)
                if first:
                    m_ref[j] = m1
                    l_ref[j] = l1
                    acc_ref[j] = ot
                else:
                    m0 = m_ref[j]
                    mn = jnp.maximum(m0, m1)
                    a = jnp.exp(m0 - mn)
                    b = jnp.exp(m1 - mn)
                    m_ref[j] = mn
                    l_ref[j] = l_ref[j] * a + l1 * b
                    acc_ref[j] = acc_ref[j] * a + ot * b
            return carry

        lax.fori_loop(0, heads_kv, one_head, 0)

    tile_step(kv_refs[0], True)
    for t in range(1, tiles):

        @pl.when(flags_ref[t] > 0)
        def _(kv_ref=kv_refs[t]):
            tile_step(kv_ref, False)

    def finish(j, carry):
        col = pl.multiple_of(j * DH, DH)
        out_ref[:, pl.ds(col, DH)] = (acc_ref[j] / l_ref[j]).T.astype(out_ref.dtype)
        return carry

    lax.fori_loop(0, heads, finish, 0)


def attend(flags, queries, pieces):
    heads = queries.shape[1] // DH
    return pl.pallas_call(
        attention_kernel,
        out_shape=jax.ShapeDtypeStruct(queries.shape, jnp.bfloat16),
        in_specs=[pl.BlockSpec(memory_space=pltpu.SMEM)]
        + [pl.BlockSpec(memory_space=pltpu.VMEM)] * (1 + len(pieces)),
        out_specs=pl.BlockSpec(memory_space=pltpu.VMEM),
        scratch_shapes=[
            pltpu.VMEM((heads, DH, queries.shape[0]), jnp.bfloat16),
            pltpu.VMEM((heads, 1, queries.shape[0]), jnp.float32),
            pltpu.VMEM((heads, 1, queries.shape[0]), jnp.float32),
            pltpu.VMEM((heads, DH, queries.shape[0]), jnp.float32),
        ],
        compiler_params=pltpu.CompilerParams(vmem_limit_bytes=56 * 1024 * 1024),
    )(flags, queries, *pieces)


def shards(queries, keys, values, lengths, class_weight):
    devices = lax.axis_size("seq")
    myself = lax.axis_index("seq")
    row_count = queries.shape[0]
    run_rows = row_count // devices
    width_q = queries.shape[1]
    width_k = keys.shape[1]
    arrived_q = lax.all_to_all(
        queries.reshape(devices, run_rows, width_q), "seq", split_axis=0, concat_axis=0, tiled=True
    )
    arrived_kv = lax.all_to_all(
        jnp.concatenate([keys, values], axis=1).reshape(devices, run_rows, 2 * width_k),
        "seq",
        split_axis=0,
        concat_axis=0,
        tiled=True,
    )
    queries = arrived_q.reshape(row_count, width_q)
    kv = arrived_kv.reshape(row_count, 2 * width_k)
    owner_doc, first_block = block_docs(lengths, devices)
    my_doc = owner_doc[myself]
    reach = MAXB - 1
    pieces = [kv]
    flags = [jnp.ones((), jnp.int32)]
    right = kv
    left = kv
    for hop in range(1, reach + 1):
        right = shifted(right, "seq", 1)
        left = shifted(left, "seq", -1)
        for piece, source in ((right, myself - hop), (left, myself + hop)):
            inside = (source >= 0) & (source < devices)
            clipped = jnp.clip(source, 0, devices - 1)
            pieces.append(piece)
            flags.append((inside & (owner_doc[clipped] == my_doc)).astype(jnp.int32))
    attended = attend(jnp.stack(flags), queries, pieces)
    own_logits = jnp.dot(attended[0:1], class_weight, preferred_element_type=jnp.float32)
    candidates = [own_logits] + [shifted(own_logits, "seq", d) for d in range(1, reach + 1)]
    distance = jnp.clip(myself - first_block[myself], 0, reach)
    doc_logits = lax.dynamic_index_in_dim(jnp.stack(candidates), distance, 0, False)
    return (attended, doc_logits)


def solution(mesh):
    return jax.shard_map(
        shards,
        mesh=mesh,
        in_specs=(P("seq", None), P("seq", None), P("seq", None), P(), P()),
        out_specs=(P("seq", None), P("seq", None)),
        check_vma=False,
    )
```

```python
import jax
import jax.numpy as jnp
from jax import lax
from jax.sharding import PartitionSpec as P
from jax.experimental import pallas as pl
from jax.experimental.pallas import tpu as pltpu

DH = 128
BLK = 128
MAXB = 8


def shifted(block, axis, distance):
    count = lax.axis_size(axis)
    if distance > 0:
        route = [(i - distance, i) for i in range(distance, count)]
    else:
        route = [(i - distance, i) for i in range(0, count + distance)]
    return lax.ppermute(block, axis, route)


def block_docs(lengths, block_count):
    doc_ends = jnp.cumsum(lengths, dtype=jnp.int32)
    doc_firsts = doc_ends - lengths
    blocks = jnp.arange(block_count, dtype=jnp.int32)
    owner_doc = jnp.sum((doc_ends[None, :] <= blocks[:, None]).astype(jnp.int32), axis=1)
    matches = owner_doc[:, None] == jnp.arange(lengths.shape[0], dtype=jnp.int32)[None, :]
    first_block = jnp.sum(jnp.where(matches, doc_firsts[None, :], 0), axis=1)
    return (owner_doc, first_block)


def attention_kernel(flags_ref, q_ref, q0t_ref, *refs):
    tiles = len(refs) - 9
    kv_refs = refs[:tiles]
    out_ref, out0_ref, qt_ref, m_ref, l_ref, acc_ref, m0_ref, l0_ref, acc0_ref = refs[tiles:]
    heads = q_ref.shape[0]
    rows = q_ref.shape[1]
    width_k = kv_refs[0].shape[1] // 2
    heads_kv = width_k // DH
    group = heads // heads_kv
    factor = DH ** (-0.5)

    def prep(j, carry):
        qt_ref[j] = q_ref[j].astype(jnp.float32).T.astype(jnp.bfloat16)
        return carry

    lax.fori_loop(0, heads, prep, 0)

    def merge(first, ms, ls, accs, j, m1, l1, o1):
        if first:
            ms[j] = m1
            ls[j] = l1
            accs[j] = o1
        else:
            m0 = ms[j]
            mn = jnp.maximum(m0, m1)
            a = jnp.exp(m0 - mn)
            b = jnp.exp(m1 - mn)
            ms[j] = mn
            ls[j] = ls[j] * a + l1 * b
            accs[j] = accs[j] * a + o1 * b

    def scored(k, vt, qt):
        st = jnp.dot(k, qt, preferred_element_type=jnp.float32) * factor
        m1 = jnp.max(st, axis=0, keepdims=True)
        p = jnp.exp(st - m1)
        l1 = jnp.sum(p, axis=0, keepdims=True)
        ot = jnp.dot(vt, p.astype(jnp.bfloat16), preferred_element_type=jnp.float32)
        return m1, l1, ot

    def tile_step(kv_ref, first):
        def one_head(h, carry):
            kcol = pl.multiple_of(h * DH, DH)
            vcol = pl.multiple_of(width_k + h * DH, DH)
            k = kv_ref[0:rows, pl.ds(kcol, DH)]
            vt = kv_ref[0:rows, pl.ds(vcol, DH)].astype(jnp.float32).T.astype(jnp.bfloat16)
            for g in range(group):
                j = h * group + g
                merge(first, m_ref, l_ref, acc_ref, j, *scored(k, vt, qt_ref[j]))
            merge(first, m0_ref, l0_ref, acc0_ref, h, *scored(k, vt, q0t_ref[h]))
            return carry

        lax.fori_loop(0, heads_kv, one_head, 0)

    tile_step(kv_refs[0], True)
    for t in range(1, tiles):

        @pl.when(flags_ref[t] > 0)
        def _(kv_ref=kv_refs[t]):
            tile_step(kv_ref, False)

    def finish(j, carry):
        col = pl.multiple_of(j * DH, DH)
        out_ref[:, pl.ds(col, DH)] = (acc_ref[j] / l_ref[j]).T.astype(out_ref.dtype)
        return carry

    lax.fori_loop(0, heads, finish, 0)
    for h in range(heads_kv):
        out0_ref[h] = acc0_ref[h] / l0_ref[h]


def attend(flags, q_heads, q0t, pieces):
    heads, rows, _ = q_heads.shape
    heads_kv = q0t.shape[0]
    width = q0t.shape[2]
    return pl.pallas_call(
        attention_kernel,
        out_shape=(
            jax.ShapeDtypeStruct((rows, heads * DH), jnp.bfloat16),
            jax.ShapeDtypeStruct((heads_kv, DH, width), jnp.float32),
        ),
        in_specs=[pl.BlockSpec(memory_space=pltpu.SMEM)]
        + [pl.BlockSpec(memory_space=pltpu.VMEM)] * (2 + len(pieces)),
        out_specs=(pl.BlockSpec(memory_space=pltpu.VMEM), pl.BlockSpec(memory_space=pltpu.VMEM)),
        scratch_shapes=[
            pltpu.VMEM((heads, DH, rows), jnp.bfloat16),
            pltpu.VMEM((heads, 1, rows), jnp.float32),
            pltpu.VMEM((heads, 1, rows), jnp.float32),
            pltpu.VMEM((heads, DH, rows), jnp.float32),
            pltpu.VMEM((heads_kv, 1, width), jnp.float32),
            pltpu.VMEM((heads_kv, 1, width), jnp.float32),
            pltpu.VMEM((heads_kv, DH, width), jnp.float32),
        ],
        compiler_params=pltpu.CompilerParams(vmem_limit_bytes=56 * 1024 * 1024),
    )(flags, q_heads, q0t, *pieces)


def shards(queries, keys, values, lengths, class_weight):
    devices = lax.axis_size("seq")
    myself = lax.axis_index("seq")
    row_count = queries.shape[0]
    width_q = queries.shape[1]
    width_k = keys.shape[1]
    heads = width_q // DH
    heads_kv = width_k // DH
    group = heads // heads_kv
    arrived_q = lax.all_to_all(
        queries.reshape(devices, heads, DH), "seq", split_axis=0, concat_axis=0, tiled=True
    )
    arrived_kv = lax.all_to_all(
        jnp.concatenate(
            [keys.reshape(devices, heads_kv, DH), values.reshape(devices, heads_kv, DH)], axis=1
        ),
        "seq",
        split_axis=0,
        concat_axis=0,
        tiled=True,
    )
    q_heads = arrived_q.transpose(1, 0, 2)
    own_q0 = arrived_q[0].reshape(-1, 2 * width_k)
    kv = jnp.concatenate([arrived_kv.reshape(row_count, 2 * width_k), own_q0], axis=0)
    owner_doc, first_block = block_docs(lengths, devices)
    my_doc = owner_doc[myself]
    reach = MAXB - 1
    pieces = [kv]
    flags = [jnp.ones((), jnp.int32)]
    firsts = [own_q0]
    right = kv
    left = kv
    for hop in range(1, reach + 1):
        right = shifted(right, "seq", 1)
        left = shifted(left, "seq", -1)
        firsts.append(right[row_count:])
        for piece, source in ((right, myself - hop), (left, myself + hop)):
            inside = (source >= 0) & (source < devices)
            clipped = jnp.clip(source, 0, devices - 1)
            pieces.append(piece)
            flags.append((inside & (owner_doc[clipped] == my_doc)).astype(jnp.int32))
    distance = jnp.clip(myself - first_block[myself], 0, reach)
    start_q0 = lax.dynamic_index_in_dim(jnp.stack(firsts), distance, 0, False)
    q0t = start_q0.reshape(heads_kv, group, DH).transpose(0, 2, 1)
    q0t = jnp.pad(q0t, ((0, 0), (0, 0), (0, DH - group)))
    attended, start_out = attend(jnp.stack(flags), q_heads, q0t, pieces)
    start_row = start_out[:, :, :group].transpose(0, 2, 1).reshape(1, width_q).astype(jnp.bfloat16)
    doc_logits = jnp.dot(start_row, class_weight, preferred_element_type=jnp.float32)
    return (attended, doc_logits)


def solution(mesh):
    return jax.shard_map(
        shards,
        mesh=mesh,
        in_specs=(P("seq", None), P("seq", None), P("seq", None), P(), P()),
        out_specs=(P("seq", None), P("seq", None)),
        check_vma=False,
    )
```

```python
import jax
import jax.numpy as jnp
from jax import lax
from jax.sharding import PartitionSpec as P
from jax.experimental import pallas as pl
from jax.experimental.pallas import tpu as pltpu

DH = 128
BLK = 128
MAXB = 8


def shifted(block, axis, distance):
    count = lax.axis_size(axis)
    if distance > 0:
        route = [(i - distance, i) for i in range(distance, count)]
    else:
        route = [(i - distance, i) for i in range(0, count + distance)]
    return lax.ppermute(block, axis, route)


def block_docs(lengths, block_count):
    doc_ends = jnp.cumsum(lengths, dtype=jnp.int32)
    doc_firsts = doc_ends - lengths
    blocks = jnp.arange(block_count, dtype=jnp.int32)
    owner_doc = jnp.sum((doc_ends[None, :] <= blocks[:, None]).astype(jnp.int32), axis=1)
    matches = owner_doc[:, None] == jnp.arange(lengths.shape[0], dtype=jnp.int32)[None, :]
    first_block = jnp.sum(jnp.where(matches, doc_firsts[None, :], 0), axis=1)
    return (owner_doc, first_block)


def attention_kernel(flags_ref, q_ref, q0t_ref, stack_ref, *refs):
    own = len(refs) - 9
    out_ref, out0_ref, qt_ref, m_ref, l_ref, acc_ref, m0_ref, l0_ref, acc0_ref = refs[own:]
    loaders = [lambda cols, r=r: r[0 : q_ref.shape[1], cols] for r in refs[:own]]
    loaders += [
        lambda cols, i=i: stack_ref[i, 0 : q_ref.shape[1], cols] for i in range(stack_ref.shape[0])
    ]
    heads = q_ref.shape[0]
    rows = q_ref.shape[1]
    width_k = stack_ref.shape[2] // 2
    heads_kv = width_k // DH
    group = heads // heads_kv
    factor = DH ** (-0.5)

    def prep(j, carry):
        qt_ref[j] = q_ref[j].astype(jnp.float32).T.astype(jnp.bfloat16)
        return carry

    lax.fori_loop(0, heads, prep, 0)

    def merge(first, ms, ls, accs, j, m1, l1, o1):
        if first:
            ms[j] = m1
            ls[j] = l1
            accs[j] = o1
        else:
            m0 = ms[j]
            mn = jnp.maximum(m0, m1)
            a = jnp.exp(m0 - mn)
            b = jnp.exp(m1 - mn)
            ms[j] = mn
            ls[j] = ls[j] * a + l1 * b
            accs[j] = accs[j] * a + o1 * b

    def scored(k, vt, qt):
        st = jnp.dot(k, qt, preferred_element_type=jnp.float32) * factor
        m1 = jnp.max(st, axis=0, keepdims=True)
        p = jnp.exp(st - m1)
        l1 = jnp.sum(p, axis=0, keepdims=True)
        ot = jnp.dot(vt, p.astype(jnp.bfloat16), preferred_element_type=jnp.float32)
        return m1, l1, ot

    def tile_step(load, first):
        def one_head(h, carry):
            kcol = pl.multiple_of(h * DH, DH)
            vcol = pl.multiple_of(width_k + h * DH, DH)
            k = load(pl.ds(kcol, DH))
            vt = load(pl.ds(vcol, DH)).astype(jnp.float32).T.astype(jnp.bfloat16)
            for g in range(group):
                j = h * group + g
                merge(first, m_ref, l_ref, acc_ref, j, *scored(k, vt, qt_ref[j]))
            merge(first, m0_ref, l0_ref, acc0_ref, h, *scored(k, vt, q0t_ref[h]))
            return carry

        lax.fori_loop(0, heads_kv, one_head, 0)

    tile_step(loaders[0], True)
    for t in range(1, len(loaders)):

        @pl.when(flags_ref[t] > 0)
        def _(load=loaders[t]):
            tile_step(load, False)

    def finish(j, carry):
        col = pl.multiple_of(j * DH, DH)
        out_ref[:, pl.ds(col, DH)] = (acc_ref[j] / l_ref[j]).T.astype(out_ref.dtype)
        return carry

    lax.fori_loop(0, heads, finish, 0)
    for h in range(heads_kv):
        out0_ref[h] = acc0_ref[h] / l0_ref[h]


def attend(flags, q_heads, q0t, partner_stack, pieces):
    heads, rows, _ = q_heads.shape
    heads_kv = q0t.shape[0]
    width = q0t.shape[2]
    return pl.pallas_call(
        attention_kernel,
        out_shape=(
            jax.ShapeDtypeStruct((rows, heads * DH), jnp.bfloat16),
            jax.ShapeDtypeStruct((heads_kv, DH, width), jnp.float32),
        ),
        in_specs=[pl.BlockSpec(memory_space=pltpu.SMEM)]
        + [pl.BlockSpec(memory_space=pltpu.VMEM)] * (3 + len(pieces)),
        out_specs=(pl.BlockSpec(memory_space=pltpu.VMEM), pl.BlockSpec(memory_space=pltpu.VMEM)),
        scratch_shapes=[
            pltpu.VMEM((heads, DH, rows), jnp.bfloat16),
            pltpu.VMEM((heads, 1, rows), jnp.float32),
            pltpu.VMEM((heads, 1, rows), jnp.float32),
            pltpu.VMEM((heads, DH, rows), jnp.float32),
            pltpu.VMEM((heads_kv, 1, width), jnp.float32),
            pltpu.VMEM((heads_kv, 1, width), jnp.float32),
            pltpu.VMEM((heads_kv, DH, width), jnp.float32),
        ],
        compiler_params=pltpu.CompilerParams(vmem_limit_bytes=56 * 1024 * 1024),
    )(flags, q_heads, q0t, partner_stack, *pieces)


def shards(queries, keys, values, lengths, class_weight):
    devices = lax.axis_size("seq")
    myself = lax.axis_index("seq")
    row_count = queries.shape[0]
    width_q = queries.shape[1]
    width_k = keys.shape[1]
    heads = width_q // DH
    heads_kv = width_k // DH
    group = heads // heads_kv
    arrived_q = lax.all_to_all(
        queries.reshape(devices, heads, DH), "seq", split_axis=0, concat_axis=0, tiled=True
    )
    arrived_kv = lax.all_to_all(
        jnp.concatenate(
            [keys.reshape(devices, heads_kv, DH), values.reshape(devices, heads_kv, DH)], axis=1
        ),
        "seq",
        split_axis=0,
        concat_axis=0,
        tiled=True,
    )
    q_heads = arrived_q.transpose(1, 0, 2)
    own_q0 = arrived_q[0].reshape(-1, 2 * width_k)
    kv = jnp.concatenate([arrived_kv.reshape(row_count, 2 * width_k), own_q0], axis=0)
    owner_doc, first_block = block_docs(lengths, devices)
    my_doc = owner_doc[myself]
    partner = myself + 1 - 2 * (myself % 2)
    pieces = [kv]
    offsets = [0]
    right = kv
    left = kv
    for hop in range(1, MAXB // 2 + 1):
        right = shifted(right, "seq", 2)
        left = shifted(left, "seq", -2)
        pieces += [right, left]
        offsets += [-2 * hop, 2 * hop]
    partner_stack = lax.ppermute(
        jnp.stack(pieces), "seq", [(i, i + 1 - 2 * (i % 2)) for i in range(devices)]
    )
    blocks = [myself + o for o in offsets] + [partner + o for o in offsets]
    flags = []
    for source in blocks:
        inside = (source >= 0) & (source < devices)
        clipped = jnp.clip(source, 0, devices - 1)
        flags.append((inside & (owner_doc[clipped] == my_doc)).astype(jnp.int32))
    flags[0] = jnp.ones((), jnp.int32)
    firsts = jnp.concatenate(
        [jnp.stack([p[row_count:] for p in pieces]), partner_stack[:, row_count:]], axis=0
    )
    picked = (jnp.stack(blocks) == first_block[myself]).astype(firsts.dtype)
    start_q0 = jnp.sum(firsts * picked[:, None, None], axis=0).astype(firsts.dtype)
    q0t = start_q0.reshape(heads_kv, group, DH).transpose(0, 2, 1)
    q0t = jnp.pad(q0t, ((0, 0), (0, 0), (0, DH - group)))
    attended, start_out = attend(jnp.stack(flags), q_heads, q0t, partner_stack, pieces)
    start_row = start_out[:, :, :group].transpose(0, 2, 1).reshape(1, width_q).astype(jnp.bfloat16)
    doc_logits = jnp.dot(start_row, class_weight, preferred_element_type=jnp.float32)
    return (attended, doc_logits)


def solution(mesh):
    return jax.shard_map(
        shards,
        mesh=mesh,
        in_specs=(P("seq", None), P("seq", None), P("seq", None), P(), P()),
        out_specs=(P("seq", None), P("seq", None)),
        check_vma=False,
    )
```

```python
import jax
import jax.numpy as jnp
from jax import lax
from jax.sharding import PartitionSpec as P
from jax.experimental import pallas as pl
from jax.experimental.pallas import tpu as pltpu

DH = 128
BLK = 128
MAXB = 8


def shifted(block, axis, distance):
    count = lax.axis_size(axis)
    if distance > 0:
        route = [(i - distance, i) for i in range(distance, count)]
    else:
        route = [(i - distance, i) for i in range(0, count + distance)]
    return lax.ppermute(block, axis, route)


def block_docs(lengths, block_count):
    doc_ends = jnp.cumsum(lengths, dtype=jnp.int32)
    doc_firsts = doc_ends - lengths
    blocks = jnp.arange(block_count, dtype=jnp.int32)
    owner_doc = jnp.sum((doc_ends[None, :] <= blocks[:, None]).astype(jnp.int32), axis=1)
    matches = owner_doc[:, None] == jnp.arange(lengths.shape[0], dtype=jnp.int32)[None, :]
    first_block = jnp.sum(jnp.where(matches, doc_firsts[None, :], 0), axis=1)
    return (owner_doc, first_block)


def attention_kernel(flags_ref, q_ref, q0t_ref, stack_ref, *refs):
    own = len(refs) - 9
    out_ref, out0_ref, qt_ref, m_ref, l_ref, acc_ref, m0_ref, l0_ref, acc0_ref = refs[own:]
    loaders = [lambda cols, r=r: r[0 : q_ref.shape[1], cols] for r in refs[:own]]
    loaders += [
        lambda cols, i=i: stack_ref[i, 0 : q_ref.shape[1], cols] for i in range(stack_ref.shape[0])
    ]
    heads = q_ref.shape[0]
    rows = q_ref.shape[1]
    width_k = stack_ref.shape[2] // 2
    heads_kv = width_k // DH
    group = heads // heads_kv
    factor = DH ** (-0.5)

    def prep(j, carry):
        qt_ref[j] = q_ref[j].astype(jnp.float32).T.astype(jnp.bfloat16)
        return carry

    lax.fori_loop(0, heads, prep, 0)

    def merge(first, ms, ls, accs, j, m1, l1, o1):
        if first:
            ms[j] = m1
            ls[j] = l1
            accs[j] = o1
        else:
            m0 = ms[j]
            mn = jnp.maximum(m0, m1)
            a = jnp.exp(m0 - mn)
            b = jnp.exp(m1 - mn)
            ms[j] = mn
            ls[j] = ls[j] * a + l1 * b
            accs[j] = accs[j] * a + o1 * b

    def scored(k, vt, qt):
        st = jnp.dot(k, qt, preferred_element_type=jnp.float32) * factor
        m1 = jnp.max(st, axis=0, keepdims=True)
        p = jnp.exp(st - m1)
        l1 = jnp.sum(p, axis=0, keepdims=True)
        ot = jnp.dot(vt, p.astype(jnp.bfloat16), preferred_element_type=jnp.float32)
        return m1, l1, ot

    def tile_step(load, first):
        def one_head(h, carry):
            kcol = pl.multiple_of(h * DH, DH)
            vcol = pl.multiple_of(width_k + h * DH, DH)
            k = load(pl.ds(kcol, DH))
            vt = load(pl.ds(vcol, DH)).astype(jnp.float32).T.astype(jnp.bfloat16)
            for g in range(group):
                j = h * group + g
                merge(first, m_ref, l_ref, acc_ref, j, *scored(k, vt, qt_ref[j]))
            merge(first, m0_ref, l0_ref, acc0_ref, h, *scored(k, vt, q0t_ref[h]))
            return carry

        lax.fori_loop(0, heads_kv, one_head, 0)

    tile_step(loaders[0], True)
    for t in range(1, len(loaders)):

        @pl.when(flags_ref[t] > 0)
        def _(load=loaders[t]):
            tile_step(load, False)

    def finish(j, carry):
        col = pl.multiple_of(j * DH, DH)
        out_ref[:, pl.ds(col, DH)] = (acc_ref[j] / l_ref[j]).T.astype(out_ref.dtype)
        return carry

    lax.fori_loop(0, heads, finish, 0)
    for h in range(heads_kv):
        out0_ref[h] = acc0_ref[h] / l0_ref[h]


def attend(flags, q_heads, q0t, partner_stack, pieces):
    heads, rows, _ = q_heads.shape
    heads_kv = q0t.shape[0]
    width = q0t.shape[2]
    return pl.pallas_call(
        attention_kernel,
        out_shape=(
            jax.ShapeDtypeStruct((rows, heads * DH), jnp.bfloat16),
            jax.ShapeDtypeStruct((heads_kv, DH, width), jnp.float32),
        ),
        in_specs=[pl.BlockSpec(memory_space=pltpu.SMEM)]
        + [pl.BlockSpec(memory_space=pltpu.VMEM)] * (3 + len(pieces)),
        out_specs=(pl.BlockSpec(memory_space=pltpu.VMEM), pl.BlockSpec(memory_space=pltpu.VMEM)),
        scratch_shapes=[
            pltpu.VMEM((heads, DH, rows), jnp.bfloat16),
            pltpu.VMEM((heads, 1, rows), jnp.float32),
            pltpu.VMEM((heads, 1, rows), jnp.float32),
            pltpu.VMEM((heads, DH, rows), jnp.float32),
            pltpu.VMEM((heads_kv, 1, width), jnp.float32),
            pltpu.VMEM((heads_kv, 1, width), jnp.float32),
            pltpu.VMEM((heads_kv, DH, width), jnp.float32),
        ],
        compiler_params=pltpu.CompilerParams(vmem_limit_bytes=56 * 1024 * 1024),
    )(flags, q_heads, q0t, partner_stack, *pieces)


def shards(queries, keys, values, lengths, class_weight):
    devices = lax.axis_size("seq")
    myself = lax.axis_index("seq")
    row_count = queries.shape[0]
    width_q = queries.shape[1]
    width_k = keys.shape[1]
    heads = width_q // DH
    heads_kv = width_k // DH
    group = heads // heads_kv
    arrived_q = lax.all_to_all(
        queries.reshape(devices, heads, DH), "seq", split_axis=0, concat_axis=0, tiled=True
    )
    arrived_kv = lax.all_to_all(
        jnp.concatenate(
            [keys.reshape(devices, heads_kv, DH), values.reshape(devices, heads_kv, DH)], axis=1
        ),
        "seq",
        split_axis=0,
        concat_axis=0,
        tiled=True,
    )
    q_heads = arrived_q.transpose(1, 0, 2)
    own_q0 = arrived_q[0].reshape(-1, 2 * width_k)
    kv = jnp.concatenate([arrived_kv.reshape(row_count, 2 * width_k), own_q0], axis=0)
    owner_doc, first_block = block_docs(lengths, devices)
    my_doc = owner_doc[myself]
    partner = myself + 1 - 2 * (myself % 2)
    pieces = [kv]
    offsets = [0]
    right = kv
    left = kv
    for hop in range(1, MAXB // 2 + 1):
        right = shifted(right, "seq", 2)
        left = shifted(left, "seq", -2)
        pieces += [right, left]
        offsets += [-2 * hop, 2 * hop]
    partner_stack = lax.ppermute(
        jnp.stack(pieces), "seq", [(i, i + 1 - 2 * (i % 2)) for i in range(devices)]
    )
    offsets = jnp.array(offsets, jnp.int32)
    blocks = jnp.concatenate([myself + offsets, partner + offsets])
    inside = (blocks >= 0) & (blocks < devices)
    docs = jnp.take(owner_doc, jnp.clip(blocks, 0, devices - 1))
    flags = (inside & (docs == my_doc)).astype(jnp.int32).at[0].set(1)
    firsts = jnp.concatenate(
        [jnp.stack([p[row_count:] for p in pieces]), partner_stack[:, row_count:]], axis=0
    )
    picked = (blocks == first_block[myself]).astype(firsts.dtype)
    start_q0 = jnp.sum(firsts * picked[:, None, None], axis=0).astype(firsts.dtype)
    q0t = start_q0.reshape(heads_kv, group, DH).transpose(0, 2, 1)
    q0t = jnp.pad(q0t, ((0, 0), (0, 0), (0, DH - group)))
    attended, start_out = attend(flags, q_heads, q0t, partner_stack, pieces)
    start_row = start_out[:, :, :group].transpose(0, 2, 1).reshape(1, width_q).astype(jnp.bfloat16)
    doc_logits = jnp.dot(start_row, class_weight, preferred_element_type=jnp.float32)
    return (attended, doc_logits)


def solution(mesh):
    return jax.shard_map(
        shards,
        mesh=mesh,
        in_specs=(P("seq", None), P("seq", None), P("seq", None), P(), P()),
        out_specs=(P("seq", None), P("seq", None)),
        check_vma=False,
    )
```

```python
import jax
import jax.numpy as jnp
from jax import lax
from jax.sharding import PartitionSpec as P
from jax.experimental import pallas as pl
from jax.experimental.pallas import tpu as pltpu

DH = 128
BLK = 128
MAXB = 8


def shifted(block, axis, distance):
    count = lax.axis_size(axis)
    if distance > 0:
        route = [(i - distance, i) for i in range(distance, count)]
    else:
        route = [(i - distance, i) for i in range(0, count + distance)]
    return lax.ppermute(block, axis, route)


def block_docs(lengths, block_count):
    doc_ends = jnp.cumsum(lengths, dtype=jnp.int32)
    doc_firsts = doc_ends - lengths
    blocks = jnp.arange(block_count, dtype=jnp.int32)
    owner_doc = jnp.sum((doc_ends[None, :] <= blocks[:, None]).astype(jnp.int32), axis=1)
    matches = owner_doc[:, None] == jnp.arange(lengths.shape[0], dtype=jnp.int32)[None, :]
    first_block = jnp.sum(jnp.where(matches, doc_firsts[None, :], 0), axis=1)
    return (owner_doc, first_block)


def attention_kernel(flags_ref, q_ref, q0t_ref, stack_ref, *refs):
    own = len(refs) - 8
    out_ref, out0_ref, m_ref, l_ref, acc_ref, m0_ref, l0_ref, acc0_ref = refs[own:]
    loaders = [lambda cols, r=r: r[0 : q_ref.shape[2], cols] for r in refs[:own]]
    loaders += [
        lambda cols, i=i: stack_ref[i, 0 : q_ref.shape[2], cols] for i in range(stack_ref.shape[0])
    ]
    heads = q_ref.shape[0]
    rows = q_ref.shape[2]
    width_k = stack_ref.shape[2] // 2
    heads_kv = width_k // DH
    group = heads // heads_kv
    factor = DH ** (-0.5)

    qt_ref = q_ref

    def merge(first, ms, ls, accs, j, m1, l1, o1):
        if first:
            ms[j] = m1
            ls[j] = l1
            accs[j] = o1
        else:
            m0 = ms[j]
            mn = jnp.maximum(m0, m1)
            a = jnp.exp(m0 - mn)
            b = jnp.exp(m1 - mn)
            ms[j] = mn
            ls[j] = ls[j] * a + l1 * b
            accs[j] = accs[j] * a + o1 * b

    def scored(k, vt, qt):
        st = jnp.dot(k, qt, preferred_element_type=jnp.float32) * factor
        m1 = jnp.max(st, axis=0, keepdims=True)
        p = jnp.exp(st - m1)
        l1 = jnp.sum(p, axis=0, keepdims=True)
        ot = jnp.dot(vt, p.astype(jnp.bfloat16), preferred_element_type=jnp.float32)
        return m1, l1, ot

    def tile_step(load, first):
        def one_head(h, carry):
            kcol = pl.multiple_of(h * DH, DH)
            vcol = pl.multiple_of(width_k + h * DH, DH)
            k = load(pl.ds(kcol, DH))
            vt = load(pl.ds(vcol, DH)).astype(jnp.float32).T.astype(jnp.bfloat16)
            for g in range(group):
                j = h * group + g
                merge(first, m_ref, l_ref, acc_ref, j, *scored(k, vt, qt_ref[j]))
            merge(first, m0_ref, l0_ref, acc0_ref, h, *scored(k, vt, q0t_ref[h]))
            return carry

        lax.fori_loop(0, heads_kv, one_head, 0)

    tile_step(loaders[0], True)
    for t in range(1, len(loaders)):

        @pl.when(flags_ref[t] > 0)
        def _(load=loaders[t]):
            tile_step(load, False)

    def finish(j, carry):
        col = pl.multiple_of(j * DH, DH)
        out_ref[:, pl.ds(col, DH)] = (acc_ref[j] / l_ref[j]).T.astype(out_ref.dtype)
        return carry

    lax.fori_loop(0, heads, finish, 0)
    for h in range(heads_kv):
        out0_ref[h] = acc0_ref[h] / l0_ref[h]


def attend(flags, q_heads, q0t, partner_stack, pieces):
    heads, _, rows = q_heads.shape
    heads_kv = q0t.shape[0]
    width = q0t.shape[2]
    return pl.pallas_call(
        attention_kernel,
        out_shape=(
            jax.ShapeDtypeStruct((rows, heads * DH), jnp.bfloat16),
            jax.ShapeDtypeStruct((heads_kv, DH, width), jnp.float32),
        ),
        in_specs=[pl.BlockSpec(memory_space=pltpu.SMEM)]
        + [pl.BlockSpec(memory_space=pltpu.VMEM)] * (3 + len(pieces)),
        out_specs=(pl.BlockSpec(memory_space=pltpu.VMEM), pl.BlockSpec(memory_space=pltpu.VMEM)),
        scratch_shapes=[
            pltpu.VMEM((heads, 1, rows), jnp.float32),
            pltpu.VMEM((heads, 1, rows), jnp.float32),
            pltpu.VMEM((heads, DH, rows), jnp.float32),
            pltpu.VMEM((heads_kv, 1, width), jnp.float32),
            pltpu.VMEM((heads_kv, 1, width), jnp.float32),
            pltpu.VMEM((heads_kv, DH, width), jnp.float32),
        ],
        compiler_params=pltpu.CompilerParams(vmem_limit_bytes=56 * 1024 * 1024),
    )(flags, q_heads, q0t, partner_stack, *pieces)


def shards(queries, keys, values, lengths, class_weight):
    devices = lax.axis_size("seq")
    myself = lax.axis_index("seq")
    row_count = queries.shape[0]
    width_q = queries.shape[1]
    width_k = keys.shape[1]
    heads = width_q // DH
    heads_kv = width_k // DH
    group = heads // heads_kv
    arrived_q = lax.all_to_all(
        queries.reshape(devices, heads, DH), "seq", split_axis=0, concat_axis=0, tiled=True
    )
    arrived_kv = lax.all_to_all(
        jnp.concatenate(
            [keys.reshape(devices, heads_kv, DH), values.reshape(devices, heads_kv, DH)], axis=1
        ),
        "seq",
        split_axis=0,
        concat_axis=0,
        tiled=True,
    )
    q_heads = arrived_q.transpose(1, 2, 0)
    own_q0 = arrived_q[0].reshape(-1, 2 * width_k)
    kv = jnp.concatenate([arrived_kv.reshape(row_count, 2 * width_k), own_q0], axis=0)
    owner_doc, first_block = block_docs(lengths, devices)
    my_doc = owner_doc[myself]
    partner = myself + 1 - 2 * (myself % 2)
    pieces = [kv]
    offsets = [0]
    right = kv
    left = kv
    for hop in range(1, MAXB // 2 + 1):
        right = shifted(right, "seq", 2)
        left = shifted(left, "seq", -2)
        pieces += [right, left]
        offsets += [-2 * hop, 2 * hop]
    partner_stack = lax.ppermute(
        jnp.stack(pieces), "seq", [(i, i + 1 - 2 * (i % 2)) for i in range(devices)]
    )
    offsets = jnp.array(offsets, jnp.int32)
    blocks = jnp.concatenate([myself + offsets, partner + offsets])
    inside = (blocks >= 0) & (blocks < devices)
    docs = jnp.take(owner_doc, jnp.clip(blocks, 0, devices - 1))
    flags = (inside & (docs == my_doc)).astype(jnp.int32).at[0].set(1)
    starts = blocks == first_block[myself]
    firsts = [p[row_count:] for p in pieces] + [partner_stack[i, row_count:] for i in range(len(pieces))]
    start_q0 = jnp.zeros_like(firsts[0])
    for t, first in enumerate(firsts):
        start_q0 = jnp.where(starts[t], first, start_q0)
    q0t = start_q0.reshape(heads_kv, group, DH).transpose(0, 2, 1)
    q0t = jnp.pad(q0t, ((0, 0), (0, 0), (0, DH - group)))
    attended, start_out = attend(flags, q_heads, q0t, partner_stack, pieces)
    start_row = start_out[:, :, :group].transpose(0, 2, 1).reshape(1, width_q).astype(jnp.bfloat16)
    doc_logits = jnp.dot(start_row, class_weight, preferred_element_type=jnp.float32)
    return (attended, doc_logits)


def solution(mesh):
    return jax.shard_map(
        shards,
        mesh=mesh,
        in_specs=(P("seq", None), P("seq", None), P("seq", None), P(), P()),
        out_specs=(P("seq", None), P("seq", None)),
        check_vma=False,
    )
```

```python
import jax
import jax.numpy as jnp
from jax import lax
from jax.sharding import PartitionSpec as P
from jax.experimental import pallas as pl
from jax.experimental.pallas import tpu as pltpu

DH = 128
BLK = 128
MAXB = 8


def shifted(block, axis, distance):
    count = lax.axis_size(axis)
    if distance > 0:
        route = [(i - distance, i) for i in range(distance, count)]
    else:
        route = [(i - distance, i) for i in range(0, count + distance)]
    return lax.ppermute(block, axis, route)


def block_docs(lengths, block_count):
    doc_ends = jnp.cumsum(lengths, dtype=jnp.int32)
    doc_firsts = doc_ends - lengths
    blocks = jnp.arange(block_count, dtype=jnp.int32)
    owner_doc = jnp.sum((doc_ends[None, :] <= blocks[:, None]).astype(jnp.int32), axis=1)
    matches = owner_doc[:, None] == jnp.arange(lengths.shape[0], dtype=jnp.int32)[None, :]
    first_block = jnp.sum(jnp.where(matches, doc_firsts[None, :], 0), axis=1)
    return (owner_doc, first_block)


def attention_kernel(meta_ref, q_ref, stack_ref, *refs):
    own = len(refs) - 8
    out_ref, out0_ref, m_ref, l_ref, acc_ref, m0_ref, l0_ref, acc0_ref = refs[own:]
    rows = q_ref.shape[2]
    loaders = [lambda cols, r=r: r[:, cols] for r in refs[:own]]
    loaders += [lambda cols, i=i: stack_ref[i, :, cols] for i in range(stack_ref.shape[0])]
    tiles = len(loaders)
    heads = q_ref.shape[0]
    width_k = (stack_ref.shape[2] - DH) // 2
    heads_kv = width_k // DH
    group = heads // heads_kv
    factor = DH ** (-0.5)
    q0s_ref = out0_ref

    for t in range(tiles):

        @pl.when(meta_ref[tiles] == t)
        def _(load=loaders[t]):
            q0s_ref[...] = load(pl.ds(2 * width_k, DH)).astype(jnp.float32)

    q0t = q0s_ref[...].astype(jnp.bfloat16)
    column_head = lax.broadcasted_iota(jnp.int32, (1, DH), 1) // group

    def scored(k, vt, qt):
        st = jnp.dot(k, qt, preferred_element_type=jnp.float32) * factor
        m1 = jnp.max(st, axis=0, keepdims=True)
        p = jnp.exp(st - m1)
        l1 = jnp.sum(p, axis=0, keepdims=True)
        ot = jnp.dot(vt, p.astype(jnp.bfloat16), preferred_element_type=jnp.float32)
        return m1, l1, ot

    def merge(first, ms, ls, accs, j, m1, l1, o1, mask=None):
        def put(ref, value):
            if mask is None:
                ref[j] = value
            else:
                ref[j] = jnp.where(mask, value, ref[j])

        if first:
            put(ms, m1)
            put(ls, l1)
            put(accs, o1)
        else:
            m0 = ms[j]
            mn = jnp.maximum(m0, m1)
            a = jnp.exp(m0 - mn)
            b = jnp.exp(m1 - mn)
            put(ms, mn)
            put(ls, ls[j] * a + l1 * b)
            put(accs, accs[j] * a + o1 * b)

    def tile_step(load, first):
        def one_head(h, carry):
            kcol = pl.multiple_of(h * DH, DH)
            vcol = pl.multiple_of(width_k + h * DH, DH)
            k = load(pl.ds(kcol, DH))
            vt = load(pl.ds(vcol, DH)).astype(jnp.float32).T.astype(jnp.bfloat16)
            for g in range(group):
                j = h * group + g
                merge(first, m_ref, l_ref, acc_ref, j, *scored(k, vt, q_ref[j]))
            merge(first, m0_ref, l0_ref, acc0_ref, 0, *scored(k, vt, q0t), mask=column_head == h)
            return carry

        lax.fori_loop(0, heads_kv, one_head, 0)

    tile_step(loaders[0], True)
    for t in range(1, tiles):

        @pl.when(meta_ref[t] > 0)
        def _(load=loaders[t]):
            tile_step(load, False)

    def finish(j, carry):
        col = pl.multiple_of(j * DH, DH)
        out_ref[:, pl.ds(col, DH)] = (acc_ref[j] / l_ref[j]).T.astype(out_ref.dtype)
        return carry

    lax.fori_loop(0, heads, finish, 0)
    out0_ref[...] = acc0_ref[0] / l0_ref[0]


def attend(meta, q_heads, partner_stack, pieces):
    heads, _, rows = q_heads.shape
    return pl.pallas_call(
        attention_kernel,
        out_shape=(
            jax.ShapeDtypeStruct((rows, heads * DH), jnp.bfloat16),
            jax.ShapeDtypeStruct((DH, DH), jnp.float32),
        ),
        in_specs=[pl.BlockSpec(memory_space=pltpu.SMEM)]
        + [pl.BlockSpec(memory_space=pltpu.VMEM)] * (2 + len(pieces)),
        out_specs=(pl.BlockSpec(memory_space=pltpu.VMEM), pl.BlockSpec(memory_space=pltpu.VMEM)),
        scratch_shapes=[
            pltpu.VMEM((heads, 1, rows), jnp.float32),
            pltpu.VMEM((heads, 1, rows), jnp.float32),
            pltpu.VMEM((heads, DH, rows), jnp.float32),
            pltpu.VMEM((1, 1, DH), jnp.float32),
            pltpu.VMEM((1, 1, DH), jnp.float32),
            pltpu.VMEM((1, DH, DH), jnp.float32),
        ],
        compiler_params=pltpu.CompilerParams(vmem_limit_bytes=56 * 1024 * 1024),
    )(meta, q_heads, partner_stack, *pieces)


def shards(queries, keys, values, lengths, class_weight):
    devices = lax.axis_size("seq")
    myself = lax.axis_index("seq")
    row_count = queries.shape[0]
    width_q = queries.shape[1]
    width_k = keys.shape[1]
    heads = width_q // DH
    heads_kv = width_k // DH
    group = heads // heads_kv
    arrived_q = lax.all_to_all(
        queries.reshape(devices, heads, DH), "seq", split_axis=0, concat_axis=0, tiled=True
    )
    arrived_kv = lax.all_to_all(
        jnp.concatenate(
            [keys.reshape(devices, heads_kv, DH), values.reshape(devices, heads_kv, DH)], axis=1
        ),
        "seq",
        split_axis=0,
        concat_axis=0,
        tiled=True,
    )
    q_heads = arrived_q.transpose(1, 2, 0)
    own_q0t = jnp.pad(arrived_q[0].T, ((0, 0), (0, DH - heads)))
    kv = jnp.concatenate([arrived_kv.reshape(row_count, 2 * width_k), own_q0t], axis=1)
    owner_doc, first_block = block_docs(lengths, devices)
    my_doc = owner_doc[myself]
    partner = myself + 1 - 2 * (myself % 2)
    pieces = [kv]
    offsets = [0]
    right = kv
    left = kv
    for hop in range(1, MAXB // 2 + 1):
        right = shifted(right, "seq", 2)
        left = shifted(left, "seq", -2)
        pieces += [right, left]
        offsets += [-2 * hop, 2 * hop]
    partner_stack = lax.ppermute(
        jnp.stack(pieces), "seq", [(i, i + 1 - 2 * (i % 2)) for i in range(devices)]
    )
    offsets = jnp.array(offsets, jnp.int32)
    blocks = jnp.concatenate([myself + offsets, partner + offsets])
    inside = (blocks >= 0) & (blocks < devices)
    docs = jnp.take(owner_doc, jnp.clip(blocks, 0, devices - 1))
    flags = (inside & (docs == my_doc)).astype(jnp.int32).at[0].set(1)
    pick = jnp.argmax(blocks == first_block[myself]).astype(jnp.int32)
    meta = jnp.concatenate([flags, pick[None]])
    attended, start_out = attend(meta, q_heads, partner_stack, pieces)
    start_row = start_out[:, :heads].T.reshape(1, width_q).astype(jnp.bfloat16)
    doc_logits = jnp.dot(start_row, class_weight, preferred_element_type=jnp.float32)
    return (attended, doc_logits)


def solution(mesh):
    return jax.shard_map(
        shards,
        mesh=mesh,
        in_specs=(P("seq", None), P("seq", None), P("seq", None), P(), P()),
        out_specs=(P("seq", None), P("seq", None)),
        check_vma=False,
    )
```

```python
import jax
import jax.numpy as jnp
from jax import lax
from jax.sharding import PartitionSpec as P
from jax.experimental import pallas as pl
from jax.experimental.pallas import tpu as pltpu

DH = 128
BLK = 128
MAXB = 8


def shifted(block, axis, distance):
    count = lax.axis_size(axis)
    if distance > 0:
        route = [(i - distance, i) for i in range(distance, count)]
    else:
        route = [(i - distance, i) for i in range(0, count + distance)]
    return lax.ppermute(block, axis, route)


def block_docs(lengths, block_count):
    doc_ends = jnp.cumsum(lengths, dtype=jnp.int32)
    doc_firsts = doc_ends - lengths
    blocks = jnp.arange(block_count, dtype=jnp.int32)
    owner_doc = jnp.sum((doc_ends[None, :] <= blocks[:, None]).astype(jnp.int32), axis=1)
    matches = owner_doc[:, None] == jnp.arange(lengths.shape[0], dtype=jnp.int32)[None, :]
    first_block = jnp.sum(jnp.where(matches, doc_firsts[None, :], 0), axis=1)
    return (owner_doc, first_block)


def attention_kernel(meta_ref, q_ref, stack_ref, *refs):
    own = len(refs) - 8
    out_ref, out0_ref, m_ref, l_ref, acc_ref, m0_ref, l0_ref, acc0_ref = refs[own:]
    rows = q_ref.shape[2]
    loaders = [lambda cols, r=r: r[:, cols] for r in refs[:own]]
    loaders += [lambda cols, i=i: stack_ref[i, :, cols] for i in range(stack_ref.shape[0])]
    tiles = len(loaders)
    heads = q_ref.shape[0]
    width_k = (stack_ref.shape[2] - DH) // 2
    heads_kv = width_k // DH
    group = heads // heads_kv
    factor = DH ** (-0.5)
    q0s_ref = out0_ref

    for t in range(tiles):

        @pl.when(meta_ref[tiles] == t)
        def _(load=loaders[t]):
            q0s_ref[...] = load(pl.ds(2 * width_k, DH)).astype(jnp.float32)

    q0t = q0s_ref[...].astype(jnp.bfloat16)
    column_head = lax.broadcasted_iota(jnp.int32, (1, DH), 1) // group

    def scored(k, vt, qt):
        st = jnp.dot(k, qt, preferred_element_type=jnp.float32) * factor
        m1 = jnp.max(st, axis=0, keepdims=True)
        p = jnp.exp(st - m1)
        l1 = jnp.sum(p, axis=0, keepdims=True)
        ot = jnp.dot(vt, p.astype(jnp.bfloat16), preferred_element_type=jnp.float32)
        return m1, l1, ot

    def merge(first, ms, ls, accs, j, m1, l1, o1, mask=None):
        def put(ref, value):
            if mask is None:
                ref[j] = value
            else:
                ref[j] = jnp.where(mask, value, ref[j])

        if first:
            put(ms, m1)
            put(ls, l1)
            put(accs, o1)
        else:
            m0 = ms[j]
            mn = jnp.maximum(m0, m1)
            a = jnp.exp(m0 - mn)
            b = jnp.exp(m1 - mn)
            put(ms, mn)
            put(ls, ls[j] * a + l1 * b)
            put(accs, accs[j] * a + o1 * b)

    def tile_step(load, first):
        def one_head(h, carry):
            kcol = pl.multiple_of(h * DH, DH)
            vcol = pl.multiple_of(width_k + h * DH, DH)
            k = load(pl.ds(kcol, DH))
            vt = load(pl.ds(vcol, DH)).astype(jnp.float32).T.astype(jnp.bfloat16)
            for g in range(group):
                j = h * group + g
                merge(first, m_ref, l_ref, acc_ref, j, *scored(k, vt, q_ref[j]))
            merge(first, m0_ref, l0_ref, acc0_ref, 0, *scored(k, vt, q0t), mask=column_head == h)
            return carry

        lax.fori_loop(0, heads_kv, one_head, 0)

    tile_step(loaders[0], True)
    for t in range(1, tiles):

        @pl.when(meta_ref[t] > 0)
        def _(load=loaders[t]):
            tile_step(load, False)

    def finish(j, carry):
        col = pl.multiple_of(j * DH, DH)
        out_ref[:, pl.ds(col, DH)] = (acc_ref[j] / l_ref[j]).T.astype(out_ref.dtype)
        return carry

    lax.fori_loop(0, heads, finish, 0)
    out0_ref[...] = acc0_ref[0] / l0_ref[0]


def attend(meta, q_heads, partner_stack, pieces):
    heads, _, rows = q_heads.shape
    return pl.pallas_call(
        attention_kernel,
        out_shape=(
            jax.ShapeDtypeStruct((rows, heads * DH), jnp.bfloat16),
            jax.ShapeDtypeStruct((DH, DH), jnp.float32),
        ),
        in_specs=[pl.BlockSpec(memory_space=pltpu.SMEM)]
        + [pl.BlockSpec(memory_space=pltpu.VMEM)] * (2 + len(pieces)),
        out_specs=(pl.BlockSpec(memory_space=pltpu.VMEM), pl.BlockSpec(memory_space=pltpu.VMEM)),
        scratch_shapes=[
            pltpu.VMEM((heads, 1, rows), jnp.float32),
            pltpu.VMEM((heads, 1, rows), jnp.float32),
            pltpu.VMEM((heads, DH, rows), jnp.float32),
            pltpu.VMEM((1, 1, DH), jnp.float32),
            pltpu.VMEM((1, 1, DH), jnp.float32),
            pltpu.VMEM((1, DH, DH), jnp.float32),
        ],
        compiler_params=pltpu.CompilerParams(vmem_limit_bytes=56 * 1024 * 1024),
    )(meta, q_heads, partner_stack, *pieces)


def shards(queries, keys, values, lengths, class_weight):
    devices = lax.axis_size("seq")
    myself = lax.axis_index("seq")
    row_count = queries.shape[0]
    width_q = queries.shape[1]
    width_k = keys.shape[1]
    heads = width_q // DH
    heads_kv = width_k // DH
    group = heads // heads_kv
    arrived = lax.all_to_all(
        jnp.concatenate(
            [
                queries.reshape(devices, heads, DH),
                keys.reshape(devices, heads_kv, DH),
                values.reshape(devices, heads_kv, DH),
            ],
            axis=1,
        ),
        "seq",
        split_axis=0,
        concat_axis=0,
        tiled=True,
    )
    owner_doc, first_block = block_docs(lengths, devices)
    my_doc = owner_doc[myself]
    partner = myself + 1 - 2 * (myself % 2)
    offsets = [0]
    for hop in range(1, MAXB // 2 + 1):
        offsets += [-2 * hop, 2 * hop]
    offsets = jnp.array(offsets, jnp.int32)
    blocks = jnp.concatenate([myself + offsets, partner + offsets])
    inside = (blocks >= 0) & (blocks < devices)
    docs = jnp.take(owner_doc, jnp.clip(blocks, 0, devices - 1))
    flags = (inside & (docs == my_doc)).astype(jnp.int32).at[0].set(1)
    pick = jnp.argmax(blocks == first_block[myself]).astype(jnp.int32)
    meta = jnp.concatenate([flags, pick[None]])
    q_heads = arrived[:, :heads].transpose(1, 2, 0)
    own_q0t = jnp.pad(arrived[0, :heads].T, ((0, 0), (0, DH - heads)))
    kv = jnp.concatenate([arrived[:, heads:].reshape(row_count, 2 * width_k), own_q0t], axis=1)
    kv, meta = lax.optimization_barrier((kv, meta))
    pieces = [kv]
    right = kv
    left = kv
    for hop in range(1, MAXB // 2 + 1):
        right = shifted(right, "seq", 2)
        left = shifted(left, "seq", -2)
        pieces += [right, left]
    partner_stack = lax.ppermute(
        jnp.stack(pieces), "seq", [(i, i + 1 - 2 * (i % 2)) for i in range(devices)]
    )
    attended, start_out = attend(meta, q_heads, partner_stack, pieces)
    start_row = start_out[:, :heads].T.reshape(1, width_q).astype(jnp.bfloat16)
    doc_logits = jnp.dot(start_row, class_weight, preferred_element_type=jnp.float32)
    return (attended, doc_logits)


def solution(mesh):
    return jax.shard_map(
        shards,
        mesh=mesh,
        in_specs=(P("seq", None), P("seq", None), P("seq", None), P(), P()),
        out_specs=(P("seq", None), P("seq", None)),
        check_vma=False,
    )
```

```python
import jax
import jax.numpy as jnp
from jax import lax
from jax.sharding import PartitionSpec as P
from jax.experimental import pallas as pl
from jax.experimental.pallas import tpu as pltpu

DH = 128
BLK = 128
MAXB = 8


def shifted(block, axis, distance):
    count = lax.axis_size(axis)
    if distance > 0:
        route = [(i - distance, i) for i in range(distance, count)]
    else:
        route = [(i - distance, i) for i in range(0, count + distance)]
    return lax.ppermute(block, axis, route)


def block_docs(lengths, block_count):
    doc_ends = jnp.cumsum(lengths, dtype=jnp.int32)
    doc_firsts = doc_ends - lengths
    blocks = jnp.arange(block_count, dtype=jnp.int32)
    owner_doc = jnp.sum((doc_ends[None, :] <= blocks[:, None]).astype(jnp.int32), axis=1)
    matches = owner_doc[:, None] == jnp.arange(lengths.shape[0], dtype=jnp.int32)[None, :]
    first_block = jnp.sum(jnp.where(matches, doc_firsts[None, :], 0), axis=1)
    return (owner_doc, first_block)


def attention_kernel(meta_ref, q_ref, stack_ref, *refs):
    own = len(refs) - 8
    out_ref, out0_ref, m_ref, l_ref, acc_ref, m0_ref, l0_ref, acc0_ref = refs[own:]
    rows = q_ref.shape[2]
    loaders = [lambda cols, r=r: r[:, cols] for r in refs[:own]]
    loaders += [lambda cols, i=i: stack_ref[i, :, cols] for i in range(stack_ref.shape[0])]
    tiles = len(loaders)
    heads = q_ref.shape[0]
    width_k = (stack_ref.shape[2] - DH) // 2
    heads_kv = width_k // DH
    group = heads // heads_kv
    factor = DH ** (-0.5)
    q0s_ref = out0_ref

    for t in range(tiles):

        @pl.when(meta_ref[tiles] == t)
        def _(load=loaders[t]):
            q0s_ref[...] = load(pl.ds(2 * width_k, DH)).astype(jnp.float32)

    q0t = q0s_ref[...].astype(jnp.bfloat16)
    column_head = lax.broadcasted_iota(jnp.int32, (1, DH), 1) // group

    def scored(k, vt, qt):
        st = jnp.dot(k, qt, preferred_element_type=jnp.float32) * factor
        m1 = jnp.max(st, axis=0, keepdims=True)
        p = jnp.exp(st - m1)
        l1 = jnp.sum(p, axis=0, keepdims=True)
        ot = jnp.dot(vt, p.astype(jnp.bfloat16), preferred_element_type=jnp.float32)
        return m1, l1, ot

    def merge(first, ms, ls, accs, j, m1, l1, o1, mask=None):
        def put(ref, value):
            if mask is None:
                ref[j] = value
            else:
                ref[j] = jnp.where(mask, value, ref[j])

        if first:
            put(ms, m1)
            put(ls, l1)
            put(accs, o1)
        else:
            m0 = ms[j]
            mn = jnp.maximum(m0, m1)
            a = jnp.exp(m0 - mn)
            b = jnp.exp(m1 - mn)
            put(ms, mn)
            put(ls, ls[j] * a + l1 * b)
            put(accs, accs[j] * a + o1 * b)

    def tile_step(load, first):
        def one_head(h, carry):
            kcol = pl.multiple_of(h * DH, DH)
            vcol = pl.multiple_of(width_k + h * DH, DH)
            k = load(pl.ds(kcol, DH))
            vt = load(pl.ds(vcol, DH)).astype(jnp.float32).T.astype(jnp.bfloat16)
            for g in range(group):
                j = h * group + g
                merge(first, m_ref, l_ref, acc_ref, j, *scored(k, vt, q_ref[j]))
            merge(first, m0_ref, l0_ref, acc0_ref, 0, *scored(k, vt, q0t), mask=column_head == h)
            return carry

        lax.fori_loop(0, heads_kv, one_head, 0)

    tile_step(loaders[0], True)
    for t in range(1, tiles):

        @pl.when(meta_ref[t] > 0)
        def _(load=loaders[t]):
            tile_step(load, False)

    def finish(j, carry):
        col = pl.multiple_of(j * DH, DH)
        out_ref[:, pl.ds(col, DH)] = (acc_ref[j] / l_ref[j]).T.astype(out_ref.dtype)
        return carry

    lax.fori_loop(0, heads, finish, 0)
    out0_ref[...] = acc0_ref[0] / l0_ref[0]


def attend(meta, q_heads, partner_stack, pieces):
    heads, _, rows = q_heads.shape
    return pl.pallas_call(
        attention_kernel,
        out_shape=(
            jax.ShapeDtypeStruct((rows, heads * DH), jnp.bfloat16),
            jax.ShapeDtypeStruct((DH, DH), jnp.float32),
        ),
        in_specs=[pl.BlockSpec(memory_space=pltpu.SMEM)]
        + [pl.BlockSpec(memory_space=pltpu.VMEM)] * (2 + len(pieces)),
        out_specs=(pl.BlockSpec(memory_space=pltpu.VMEM), pl.BlockSpec(memory_space=pltpu.VMEM)),
        scratch_shapes=[
            pltpu.VMEM((heads, 1, rows), jnp.float32),
            pltpu.VMEM((heads, 1, rows), jnp.float32),
            pltpu.VMEM((heads, DH, rows), jnp.float32),
            pltpu.VMEM((1, 1, DH), jnp.float32),
            pltpu.VMEM((1, 1, DH), jnp.float32),
            pltpu.VMEM((1, DH, DH), jnp.float32),
        ],
        compiler_params=pltpu.CompilerParams(vmem_limit_bytes=56 * 1024 * 1024),
    )(meta, q_heads, partner_stack, *pieces)


def shards(queries, keys, values, lengths, class_weight):
    devices = lax.axis_size("seq")
    myself = lax.axis_index("seq")
    row_count = queries.shape[0]
    width_q = queries.shape[1]
    width_k = keys.shape[1]
    heads = width_q // DH
    heads_kv = width_k // DH
    group = heads // heads_kv
    arrived = lax.all_to_all(
        jnp.concatenate(
            [
                queries.reshape(devices, heads, DH),
                keys.reshape(devices, heads_kv, DH),
                values.reshape(devices, heads_kv, DH),
            ],
            axis=1,
        ),
        "seq",
        split_axis=0,
        concat_axis=0,
        tiled=True,
    )
    owner_doc, first_block = block_docs(lengths, devices)
    my_doc = owner_doc[myself]
    partner = myself + 1 - 2 * (myself % 2)
    hops = MAXB // 2
    offsets = [0]
    for hop in range(1, hops):
        offsets += [-2 * hop, 2 * hop]
    offsets = jnp.array(offsets + [0], jnp.int32)
    last = jnp.array([0] * (2 * hops - 1) + [2 * hops], jnp.int32)
    blocks = jnp.concatenate(
        [myself + offsets + last * (1 - 2 * (myself % 2)), partner + offsets + last * (1 - 2 * (partner % 2))]
    )
    inside = (blocks >= 0) & (blocks < devices)
    docs = jnp.take(owner_doc, jnp.clip(blocks, 0, devices - 1))
    flags = (inside & (docs == my_doc)).astype(jnp.int32).at[0].set(1)
    pick = jnp.argmax(blocks == first_block[myself]).astype(jnp.int32)
    meta = jnp.concatenate([flags, pick[None]])
    q_heads = arrived[:, :heads].transpose(1, 2, 0)
    own_q0t = jnp.pad(arrived[0, :heads].T, ((0, 0), (0, DH - heads)))
    kv = jnp.concatenate([arrived[:, heads:].reshape(row_count, 2 * width_k), own_q0t], axis=1)
    kv, meta = lax.optimization_barrier((kv, meta))
    pieces = [kv]
    right = kv
    left = kv
    for hop in range(1, hops):
        right = shifted(right, "seq", 2)
        left = shifted(left, "seq", -2)
        pieces += [right, left]
    onward = jnp.where(myself % 2 == 1, right, left)
    route = [(i, i + 2) for i in range(1, devices - 2, 2)] + [(i, i - 2) for i in range(2, devices, 2)]
    pieces.append(lax.ppermute(onward, "seq", route))
    partner_stack = lax.ppermute(
        jnp.stack(pieces), "seq", [(i, i + 1 - 2 * (i % 2)) for i in range(devices)]
    )
    attended, start_out = attend(meta, q_heads, partner_stack, pieces)
    start_row = start_out[:, :heads].T.reshape(1, width_q).astype(jnp.bfloat16)
    doc_logits = jnp.dot(start_row, class_weight, preferred_element_type=jnp.float32)
    return (attended, doc_logits)


def solution(mesh):
    return jax.shard_map(
        shards,
        mesh=mesh,
        in_specs=(P("seq", None), P("seq", None), P("seq", None), P(), P()),
        out_specs=(P("seq", None), P("seq", None)),
        check_vma=False,
    )
```

```python
import jax
import jax.numpy as jnp
from jax import lax
from jax.sharding import PartitionSpec as P
from jax.experimental import pallas as pl
from jax.experimental.pallas import tpu as pltpu

DH = 128
BLK = 128
MAXB = 8


def shifted(block, axis, distance):
    count = lax.axis_size(axis)
    if distance > 0:
        route = [(i - distance, i) for i in range(distance, count)]
    else:
        route = [(i - distance, i) for i in range(0, count + distance)]
    return lax.ppermute(block, axis, route)


def block_docs(lengths, block_count):
    doc_ends = jnp.cumsum(lengths, dtype=jnp.int32)
    doc_firsts = doc_ends - lengths
    blocks = jnp.arange(block_count, dtype=jnp.int32)
    owner_doc = jnp.sum((doc_ends[None, :] <= blocks[:, None]).astype(jnp.int32), axis=1)
    matches = owner_doc[:, None] == jnp.arange(lengths.shape[0], dtype=jnp.int32)[None, :]
    first_block = jnp.sum(jnp.where(matches, doc_firsts[None, :], 0), axis=1)
    return (owner_doc, first_block)


def attention_kernel(meta_ref, q_ref, stack_ref, *refs):
    own = len(refs) - 8
    out_ref, out0_ref, m_ref, l_ref, acc_ref, m0_ref, l0_ref, acc0_ref = refs[own:]
    rows = q_ref.shape[2]
    loaders = [lambda cols, r=r: r[:, cols] for r in refs[:own]]
    loaders += [lambda cols, i=i: stack_ref[i, :, cols] for i in range(stack_ref.shape[0])]
    tiles = len(loaders)
    heads = q_ref.shape[0]
    width_k = (stack_ref.shape[2] - DH) // 2
    heads_kv = width_k // DH
    group = heads // heads_kv
    factor = DH ** (-0.5)
    q0s_ref = out0_ref

    for t in range(tiles):

        @pl.when(meta_ref[tiles] == t)
        def _(load=loaders[t]):
            q0s_ref[...] = load(pl.ds(2 * width_k, DH)).astype(jnp.float32)

    q0t = q0s_ref[...].astype(jnp.bfloat16)
    column_head = lax.broadcasted_iota(jnp.int32, (1, DH), 1) // group

    def scored(k, vt, qt):
        st = jnp.dot(k, qt, preferred_element_type=jnp.float32) * factor
        m1 = jnp.max(st, axis=0, keepdims=True)
        p = jnp.exp(st - m1)
        l1 = jnp.sum(p, axis=0, keepdims=True)
        ot = jnp.dot(vt, p.astype(jnp.bfloat16), preferred_element_type=jnp.float32)
        return m1, l1, ot

    def merge(first, ms, ls, accs, j, m1, l1, o1, mask=None):
        def put(ref, value):
            if mask is None:
                ref[j] = value
            else:
                ref[j] = jnp.where(mask, value, ref[j])

        if first:
            put(ms, m1)
            put(ls, l1)
            put(accs, o1)
        else:
            m0 = ms[j]
            mn = jnp.maximum(m0, m1)
            a = jnp.exp(m0 - mn)
            b = jnp.exp(m1 - mn)
            put(ms, mn)
            put(ls, ls[j] * a + l1 * b)
            put(accs, accs[j] * a + o1 * b)

    def tile_step(load, first):
        def one_head(h, carry):
            kcol = pl.multiple_of(h * DH, DH)
            vcol = pl.multiple_of(width_k + h * DH, DH)
            k = load(pl.ds(kcol, DH))
            vt = load(pl.ds(vcol, DH)).astype(jnp.float32).T.astype(jnp.bfloat16)
            for g in range(group):
                j = h * group + g
                merge(first, m_ref, l_ref, acc_ref, j, *scored(k, vt, q_ref[j]))
            merge(first, m0_ref, l0_ref, acc0_ref, 0, *scored(k, vt, q0t), mask=column_head == h)
            return carry

        lax.fori_loop(0, heads_kv, one_head, 0)

    tile_step(loaders[0], True)
    for t in range(1, tiles):

        @pl.when(meta_ref[t] > 0)
        def _(load=loaders[t]):
            tile_step(load, False)

    def finish(j, carry):
        col = pl.multiple_of(j * DH, DH)
        out_ref[:, pl.ds(col, DH)] = (acc_ref[j] / l_ref[j]).T.astype(out_ref.dtype)
        return carry

    lax.fori_loop(0, heads, finish, 0)
    out0_ref[...] = acc0_ref[0] / l0_ref[0]


def attend(meta, q_heads, partner_stack, pieces):
    heads, _, rows = q_heads.shape
    return pl.pallas_call(
        attention_kernel,
        out_shape=(
            jax.ShapeDtypeStruct((rows, heads * DH), jnp.bfloat16),
            jax.ShapeDtypeStruct((DH, DH), jnp.float32),
        ),
        in_specs=[pl.BlockSpec(memory_space=pltpu.SMEM)]
        + [pl.BlockSpec(memory_space=pltpu.VMEM)] * (2 + len(pieces)),
        out_specs=(pl.BlockSpec(memory_space=pltpu.VMEM), pl.BlockSpec(memory_space=pltpu.VMEM)),
        scratch_shapes=[
            pltpu.VMEM((heads, 1, rows), jnp.float32),
            pltpu.VMEM((heads, 1, rows), jnp.float32),
            pltpu.VMEM((heads, DH, rows), jnp.float32),
            pltpu.VMEM((1, 1, DH), jnp.float32),
            pltpu.VMEM((1, 1, DH), jnp.float32),
            pltpu.VMEM((1, DH, DH), jnp.float32),
        ],
        compiler_params=pltpu.CompilerParams(vmem_limit_bytes=56 * 1024 * 1024),
    )(meta, q_heads, partner_stack, *pieces)


def shards(queries, keys, values, lengths, class_weight):
    devices = lax.axis_size("seq")
    myself = lax.axis_index("seq")
    row_count = queries.shape[0]
    width_q = queries.shape[1]
    width_k = keys.shape[1]
    heads = width_q // DH
    heads_kv = width_k // DH
    group = heads // heads_kv
    arrived = lax.all_to_all(
        jnp.concatenate(
            [
                queries.reshape(devices, heads, DH),
                keys.reshape(devices, heads_kv, DH),
                values.reshape(devices, heads_kv, DH),
            ],
            axis=1,
        ),
        "seq",
        split_axis=0,
        concat_axis=0,
        tiled=True,
    )
    owner_doc, first_block = block_docs(lengths, devices)
    my_doc = owner_doc[myself]
    partner = myself + 1 - 2 * (myself % 2)
    hops = MAXB // 2
    offsets = [0]
    for hop in range(1, hops):
        offsets += [-2 * hop, 2 * hop]
    offsets = jnp.array(offsets + [0], jnp.int32)
    last = jnp.array([0] * (2 * hops - 1) + [2 * hops], jnp.int32)
    blocks = jnp.concatenate(
        [myself + offsets + last * (1 - 2 * (myself % 2)), partner + offsets + last * (1 - 2 * (partner % 2))]
    )
    inside = (blocks >= 0) & (blocks < devices)
    docs = jnp.take(owner_doc, jnp.clip(blocks, 0, devices - 1))
    flags = (inside & (docs == my_doc)).astype(jnp.int32).at[0].set(1)
    pick = jnp.argmax(blocks == first_block[myself]).astype(jnp.int32)
    meta = jnp.concatenate([flags, pick[None]])
    q_heads = arrived[:, :heads].transpose(1, 2, 0)
    own_q0t = jnp.pad(arrived[0, :heads].T, ((0, 0), (0, DH - heads)))
    kv = jnp.concatenate([arrived[:, heads:].reshape(row_count, 2 * width_k), own_q0t], axis=1)
    kv, meta = lax.optimization_barrier((kv, meta))
    pieces = [kv]
    right = kv
    left = kv
    for hop in range(1, hops):
        right = shifted(right, "seq", 2)
        left = shifted(left, "seq", -2)
        if hop == 1:
            right, left, q_heads = lax.optimization_barrier((right, left, q_heads))
        pieces += [right, left]
    onward = jnp.where(myself % 2 == 1, right, left)
    route = [(i, i + 2) for i in range(1, devices - 2, 2)] + [(i, i - 2) for i in range(2, devices, 2)]
    pieces.append(lax.ppermute(onward, "seq", route))
    partner_stack = lax.ppermute(
        jnp.stack(pieces), "seq", [(i, i + 1 - 2 * (i % 2)) for i in range(devices)]
    )
    attended, start_out = attend(meta, q_heads, partner_stack, pieces)
    start_row = start_out[:, :heads].T.reshape(1, width_q).astype(jnp.bfloat16)
    doc_logits = jnp.dot(start_row, class_weight, preferred_element_type=jnp.float32)
    return (attended, doc_logits)


def solution(mesh):
    return jax.shard_map(
        shards,
        mesh=mesh,
        in_specs=(P("seq", None), P("seq", None), P("seq", None), P(), P()),
        out_specs=(P("seq", None), P("seq", None)),
        check_vma=False,
    )
```

```python
import jax
import jax.numpy as jnp
from jax import lax
from jax.sharding import PartitionSpec as P
from jax.experimental import pallas as pl
from jax.experimental.pallas import tpu as pltpu

DH = 128
BLK = 128
MAXB = 8


def shifted(block, axis, distance):
    count = lax.axis_size(axis)
    if distance > 0:
        route = [(i - distance, i) for i in range(distance, count)]
    else:
        route = [(i - distance, i) for i in range(0, count + distance)]
    return lax.ppermute(block, axis, route)


def block_docs(lengths, block_count):
    doc_ends = jnp.cumsum(lengths, dtype=jnp.int32)
    doc_firsts = doc_ends - lengths
    blocks = jnp.arange(block_count, dtype=jnp.int32)
    owner_doc = jnp.sum((doc_ends[None, :] <= blocks[:, None]).astype(jnp.int32), axis=1)
    matches = owner_doc[:, None] == jnp.arange(lengths.shape[0], dtype=jnp.int32)[None, :]
    first_block = jnp.sum(jnp.where(matches, doc_firsts[None, :], 0), axis=1)
    return (owner_doc, first_block)


def attention_kernel(meta_ref, q_ref, stack_ref, *refs):
    own = len(refs) - 4
    out_ref, m_ref, l_ref, acc_ref = refs[own:]
    rows = q_ref.shape[2]
    loaders = [lambda cols, r=r: r[:, cols] for r in refs[:own]]
    loaders += [lambda cols, i=i: stack_ref[i, :, cols] for i in range(stack_ref.shape[0])]
    tiles = len(loaders)
    heads = q_ref.shape[0]
    width_k = stack_ref.shape[2] // 2
    heads_kv = width_k // DH
    group = heads // heads_kv
    factor = DH ** (-0.5)
    def scored(k, vt, qt):
        st = jnp.dot(k, qt, preferred_element_type=jnp.float32) * factor
        m1 = jnp.max(st, axis=0, keepdims=True)
        p = jnp.exp(st - m1)
        l1 = jnp.sum(p, axis=0, keepdims=True)
        ot = jnp.dot(vt, p.astype(jnp.bfloat16), preferred_element_type=jnp.float32)
        return m1, l1, ot

    def merge(first, ms, ls, accs, j, m1, l1, o1, mask=None):
        def put(ref, value):
            if mask is None:
                ref[j] = value
            else:
                ref[j] = jnp.where(mask, value, ref[j])

        if first:
            put(ms, m1)
            put(ls, l1)
            put(accs, o1)
        else:
            m0 = ms[j]
            mn = jnp.maximum(m0, m1)
            a = jnp.exp(m0 - mn)
            b = jnp.exp(m1 - mn)
            put(ms, mn)
            put(ls, ls[j] * a + l1 * b)
            put(accs, accs[j] * a + o1 * b)

    def tile_step(load, first):
        def one_head(h, carry):
            kcol = pl.multiple_of(h * DH, DH)
            vcol = pl.multiple_of(width_k + h * DH, DH)
            k = load(pl.ds(kcol, DH))
            vt = load(pl.ds(vcol, DH)).astype(jnp.float32).T.astype(jnp.bfloat16)
            for g in range(group):
                j = h * group + g
                merge(first, m_ref, l_ref, acc_ref, j, *scored(k, vt, q_ref[j]))
            return carry

        lax.fori_loop(0, heads_kv, one_head, 0)

    tile_step(loaders[0], True)
    for t in range(1, tiles):

        @pl.when(meta_ref[t] > 0)
        def _(load=loaders[t]):
            tile_step(load, False)

    def finish(j, carry):
        col = pl.multiple_of(j * DH, DH)
        out_ref[:, pl.ds(col, DH)] = (acc_ref[j] / l_ref[j]).T.astype(out_ref.dtype)
        return carry

    lax.fori_loop(0, heads, finish, 0)


def attend(meta, q_heads, partner_stack, pieces):
    heads, _, rows = q_heads.shape
    return pl.pallas_call(
        attention_kernel,
        out_shape=jax.ShapeDtypeStruct((rows, heads * DH), jnp.bfloat16),
        in_specs=[pl.BlockSpec(memory_space=pltpu.SMEM)]
        + [pl.BlockSpec(memory_space=pltpu.VMEM)] * (2 + len(pieces)),
        out_specs=pl.BlockSpec(memory_space=pltpu.VMEM),
        scratch_shapes=[
            pltpu.VMEM((heads, 1, rows), jnp.float32),
            pltpu.VMEM((heads, 1, rows), jnp.float32),
            pltpu.VMEM((heads, DH, rows), jnp.float32),
        ],
        compiler_params=pltpu.CompilerParams(vmem_limit_bytes=56 * 1024 * 1024),
    )(meta, q_heads, partner_stack, *pieces)


def shards(queries, keys, values, lengths, class_weight):
    devices = lax.axis_size("seq")
    myself = lax.axis_index("seq")
    row_count = queries.shape[0]
    width_q = queries.shape[1]
    width_k = keys.shape[1]
    heads = width_q // DH
    heads_kv = width_k // DH
    group = heads // heads_kv
    arrived_kv = lax.all_to_all(
        jnp.concatenate(
            [keys.reshape(devices, heads_kv, DH), values.reshape(devices, heads_kv, DH)], axis=1
        ),
        "seq",
        split_axis=0,
        concat_axis=0,
        tiled=True,
    )
    arrived_q = lax.all_to_all(
        queries.reshape(devices, heads, DH), "seq", split_axis=0, concat_axis=0, tiled=True
    )
    owner_doc, first_block = block_docs(lengths, devices)
    my_doc = owner_doc[myself]
    partner = myself + 1 - 2 * (myself % 2)
    hops = MAXB // 2
    offsets = [0]
    for hop in range(1, hops):
        offsets += [-2 * hop, 2 * hop]
    offsets = jnp.array(offsets + [0], jnp.int32)
    last = jnp.array([0] * (2 * hops - 1) + [2 * hops], jnp.int32)
    blocks = jnp.concatenate(
        [
            myself + offsets + last * (1 - 2 * (myself % 2)),
            partner + offsets + last * (1 - 2 * (partner % 2)),
        ]
    )
    inside = (blocks >= 0) & (blocks < devices)
    docs = jnp.take(owner_doc, jnp.clip(blocks, 0, devices - 1))
    flags = (inside & (docs == my_doc)).astype(jnp.int32).at[0].set(1)
    kv = arrived_kv.reshape(row_count, 2 * width_k)
    kv, flags = lax.optimization_barrier((kv, flags))
    pieces = [kv]
    right = kv
    left = kv
    for hop in range(1, hops):
        right = shifted(right, "seq", 2)
        left = shifted(left, "seq", -2)
        pieces += [right, left]
    onward = jnp.where(myself % 2 == 1, right, left)
    route = [(i, i + 2) for i in range(1, devices - 2, 2)] + [(i, i - 2) for i in range(2, devices, 2)]
    pieces.append(lax.ppermute(onward, "seq", route))
    partner_stack = lax.ppermute(
        jnp.stack(pieces), "seq", [(i, i + 1 - 2 * (i % 2)) for i in range(devices)]
    )
    q_heads = arrived_q.transpose(1, 2, 0)
    attended = attend(flags, q_heads, partner_stack, pieces)
    own_logits = jnp.dot(attended[0:1], class_weight, preferred_element_type=jnp.float32)
    opening = (first_block[myself] == myself).astype(jnp.float32).reshape(1, 1)
    state = jnp.concatenate([own_logits, opening], axis=1)
    distance = 1
    while distance < MAXB:
        behind = shifted(state, "seq", distance)
        state = jnp.where(state[:, -1:] > 0, state, behind)
        distance *= 2
    doc_logits = state[:, :-1]
    return (attended, doc_logits)


def solution(mesh):
    return jax.shard_map(
        shards,
        mesh=mesh,
        in_specs=(P("seq", None), P("seq", None), P("seq", None), P(), P()),
        out_specs=(P("seq", None), P("seq", None)),
        check_vma=False,
    )
```

```python
import jax
import jax.numpy as jnp
from jax import lax
from jax.sharding import PartitionSpec as P
from jax.experimental import pallas as pl
from jax.experimental.pallas import tpu as pltpu

DH = 128
BLK = 128
MAXB = 8


def shifted(block, axis, distance):
    count = lax.axis_size(axis)
    if distance > 0:
        route = [(i - distance, i) for i in range(distance, count)]
    else:
        route = [(i - distance, i) for i in range(0, count + distance)]
    return lax.ppermute(block, axis, route)


def block_docs(lengths, block_count):
    doc_ends = jnp.cumsum(lengths, dtype=jnp.int32)
    doc_firsts = doc_ends - lengths
    blocks = jnp.arange(block_count, dtype=jnp.int32)
    owner_doc = jnp.sum((doc_ends[None, :] <= blocks[:, None]).astype(jnp.int32), axis=1)
    matches = owner_doc[:, None] == jnp.arange(lengths.shape[0], dtype=jnp.int32)[None, :]
    first_block = jnp.sum(jnp.where(matches, doc_firsts[None, :], 0), axis=1)
    return (owner_doc, first_block)


def attention_kernel(meta_ref, q_ref, stack_ref, *refs):
    own = len(refs) - 8
    out_ref, out0_ref, m_ref, l_ref, acc_ref, m0_ref, l0_ref, acc0_ref = refs[own:]
    rows = q_ref.shape[2] // 2
    loaders = [lambda cols, r=r: r[:, cols] for r in refs[:own]]
    loaders += [lambda cols, i=i: stack_ref[i, :, cols] for i in range(stack_ref.shape[0])]
    tiles = len(loaders)
    heads = 2 * q_ref.shape[0]
    width_k = (stack_ref.shape[2] - DH) // 2
    heads_kv = width_k // DH
    group = heads // heads_kv
    factor = DH ** (-0.5)
    q0s_ref = out0_ref

    for t in range(tiles):

        @pl.when(meta_ref[tiles] == t)
        def _(load=loaders[t]):
            q0s_ref[...] = load(pl.ds(2 * width_k, DH)).astype(jnp.float32)

    q0t = q0s_ref[...].astype(jnp.bfloat16)
    column_head = lax.broadcasted_iota(jnp.int32, (1, DH), 1) // group

    def scored(k, vt, qt):
        st = jnp.dot(k, qt, preferred_element_type=jnp.float32) * factor
        m1 = jnp.max(st, axis=0, keepdims=True)
        p = jnp.exp(st - m1)
        l1 = jnp.sum(p, axis=0, keepdims=True)
        ot = jnp.dot(vt, p.astype(jnp.bfloat16), preferred_element_type=jnp.float32)
        return m1, l1, ot

    def merge(first, ms, ls, accs, j, m1, l1, o1, mask=None):
        def put(ref, value):
            if mask is None:
                ref[j] = value
            else:
                ref[j] = jnp.where(mask, value, ref[j])

        if first:
            put(ms, m1)
            put(ls, l1)
            put(accs, o1)
        else:
            m0 = ms[j]
            mn = jnp.maximum(m0, m1)
            a = jnp.exp(m0 - mn)
            b = jnp.exp(m1 - mn)
            put(ms, mn)
            put(ls, ls[j] * a + l1 * b)
            put(accs, accs[j] * a + o1 * b)

    def tile_step(load, first):
        def one_head(h, carry):
            kcol = pl.multiple_of(h * DH, DH)
            vcol = pl.multiple_of(width_k + h * DH, DH)
            k = load(pl.ds(kcol, DH))
            vt = load(pl.ds(vcol, DH)).astype(jnp.float32).T.astype(jnp.bfloat16)
            for g in range(group // 2):
                j = h * (group // 2) + g
                merge(first, m_ref, l_ref, acc_ref, j, *scored(k, vt, q_ref[j]))
            merge(first, m0_ref, l0_ref, acc0_ref, 0, *scored(k, vt, q0t), mask=column_head == h)
            return carry

        lax.fori_loop(0, heads_kv, one_head, 0)

    tile_step(loaders[0], True)
    for t in range(1, tiles):

        @pl.when(meta_ref[t] > 0)
        def _(load=loaders[t]):
            tile_step(load, False)

    def finish(j, carry):
        normed = (acc_ref[j] / l_ref[j]).T.astype(out_ref.dtype)
        out_ref[:, pl.ds(pl.multiple_of(2 * j * DH, DH), DH)] = normed[:rows]
        out_ref[:, pl.ds(pl.multiple_of((2 * j + 1) * DH, DH), DH)] = normed[rows:]
        return carry

    lax.fori_loop(0, heads // 2, finish, 0)
    out0_ref[...] = acc0_ref[0] / l0_ref[0]


def attend(meta, q_heads, partner_stack, pieces):
    heads, _, rows = q_heads.shape
    heads, rows = 2 * heads, rows // 2
    return pl.pallas_call(
        attention_kernel,
        out_shape=(
            jax.ShapeDtypeStruct((rows, heads * DH), jnp.bfloat16),
            jax.ShapeDtypeStruct((DH, DH), jnp.float32),
        ),
        in_specs=[pl.BlockSpec(memory_space=pltpu.SMEM)]
        + [pl.BlockSpec(memory_space=pltpu.VMEM)] * (2 + len(pieces)),
        out_specs=(pl.BlockSpec(memory_space=pltpu.VMEM), pl.BlockSpec(memory_space=pltpu.VMEM)),
        scratch_shapes=[
            pltpu.VMEM((heads // 2, 1, 2 * rows), jnp.float32),
            pltpu.VMEM((heads // 2, 1, 2 * rows), jnp.float32),
            pltpu.VMEM((heads // 2, DH, 2 * rows), jnp.float32),
            pltpu.VMEM((1, 1, DH), jnp.float32),
            pltpu.VMEM((1, 1, DH), jnp.float32),
            pltpu.VMEM((1, DH, DH), jnp.float32),
        ],
        compiler_params=pltpu.CompilerParams(vmem_limit_bytes=56 * 1024 * 1024),
    )(meta, q_heads, partner_stack, *pieces)


def shards(queries, keys, values, lengths, class_weight):
    devices = lax.axis_size("seq")
    myself = lax.axis_index("seq")
    row_count = queries.shape[0]
    width_q = queries.shape[1]
    width_k = keys.shape[1]
    heads = width_q // DH
    heads_kv = width_k // DH
    group = heads // heads_kv
    arrived = lax.all_to_all(
        jnp.concatenate(
            [
                queries.reshape(devices, heads, DH),
                keys.reshape(devices, heads_kv, DH),
                values.reshape(devices, heads_kv, DH),
            ],
            axis=1,
        ),
        "seq",
        split_axis=0,
        concat_axis=0,
        tiled=True,
    )
    owner_doc, first_block = block_docs(lengths, devices)
    my_doc = owner_doc[myself]
    partner = myself + 1 - 2 * (myself % 2)
    hops = MAXB // 2
    offsets = [0]
    for hop in range(1, hops):
        offsets += [-2 * hop, 2 * hop]
    offsets = jnp.array(offsets + [0], jnp.int32)
    last = jnp.array([0] * (2 * hops - 1) + [2 * hops], jnp.int32)
    blocks = jnp.concatenate(
        [myself + offsets + last * (1 - 2 * (myself % 2)), partner + offsets + last * (1 - 2 * (partner % 2))]
    )
    inside = (blocks >= 0) & (blocks < devices)
    docs = jnp.take(owner_doc, jnp.clip(blocks, 0, devices - 1))
    flags = (inside & (docs == my_doc)).astype(jnp.int32).at[0].set(1)
    pick = jnp.argmax(blocks == first_block[myself]).astype(jnp.int32)
    meta = jnp.concatenate([flags, pick[None]])
    q_heads = (
        arrived[:, :heads]
        .reshape(row_count, heads // 2, 2, DH)
        .transpose(1, 3, 2, 0)
        .reshape(heads // 2, DH, 2 * row_count)
    )
    own_q0t = jnp.pad(arrived[0, :heads].T, ((0, 0), (0, DH - heads)))
    kv = jnp.concatenate([arrived[:, heads:].reshape(row_count, 2 * width_k), own_q0t], axis=1)
    kv, meta = lax.optimization_barrier((kv, meta))
    pieces = [kv]
    right = kv
    left = kv
    for hop in range(1, hops):
        right = shifted(right, "seq", 2)
        left = shifted(left, "seq", -2)
        pieces += [right, left]
    onward = jnp.where(myself % 2 == 1, right, left)
    route = [(i, i + 2) for i in range(1, devices - 2, 2)] + [(i, i - 2) for i in range(2, devices, 2)]
    pieces.append(lax.ppermute(onward, "seq", route))
    partner_stack = lax.ppermute(
        jnp.stack(pieces), "seq", [(i, i + 1 - 2 * (i % 2)) for i in range(devices)]
    )
    attended, start_out = attend(meta, q_heads, partner_stack, pieces)
    start_row = start_out[:, :heads].T.reshape(1, width_q).astype(jnp.bfloat16)
    doc_logits = jnp.dot(start_row, class_weight, preferred_element_type=jnp.float32)
    return (attended, doc_logits)


def solution(mesh):
    return jax.shard_map(
        shards,
        mesh=mesh,
        in_specs=(P("seq", None), P("seq", None), P("seq", None), P(), P()),
        out_specs=(P("seq", None), P("seq", None)),
        check_vma=False,
    )
```

```python
import jax
import jax.numpy as jnp
from jax import lax
from jax.sharding import PartitionSpec as P
from jax.experimental import pallas as pl
from jax.experimental.pallas import tpu as pltpu

DH = 128
PACK = 4
BLK = 128
MAXB = 8


def shifted(block, axis, distance):
    count = lax.axis_size(axis)
    if distance > 0:
        route = [(i - distance, i) for i in range(distance, count)]
    else:
        route = [(i - distance, i) for i in range(0, count + distance)]
    return lax.ppermute(block, axis, route)


def block_docs(lengths, block_count):
    doc_ends = jnp.cumsum(lengths, dtype=jnp.int32)
    doc_firsts = doc_ends - lengths
    blocks = jnp.arange(block_count, dtype=jnp.int32)
    owner_doc = jnp.sum((doc_ends[None, :] <= blocks[:, None]).astype(jnp.int32), axis=1)
    matches = owner_doc[:, None] == jnp.arange(lengths.shape[0], dtype=jnp.int32)[None, :]
    first_block = jnp.sum(jnp.where(matches, doc_firsts[None, :], 0), axis=1)
    return (owner_doc, first_block)


def attention_kernel(meta_ref, q_ref, stack_ref, *refs):
    own = len(refs) - 8
    out_ref, out0_ref, m_ref, l_ref, acc_ref, m0_ref, l0_ref, acc0_ref = refs[own:]
    rows = q_ref.shape[2] // PACK
    loaders = [lambda cols, r=r: r[:, cols] for r in refs[:own]]
    loaders += [lambda cols, i=i: stack_ref[i, :, cols] for i in range(stack_ref.shape[0])]
    tiles = len(loaders)
    heads = PACK * q_ref.shape[0]
    width_k = (stack_ref.shape[2] - DH) // 2
    heads_kv = width_k // DH
    group = heads // heads_kv
    factor = DH ** (-0.5)
    q0s_ref = out0_ref

    for t in range(tiles):

        @pl.when(meta_ref[tiles] == t)
        def _(load=loaders[t]):
            q0s_ref[...] = load(pl.ds(2 * width_k, DH)).astype(jnp.float32)

    q0t = q0s_ref[...].astype(jnp.bfloat16)
    column_head = lax.broadcasted_iota(jnp.int32, (1, DH), 1) // group

    def scored(k, vt, qt):
        st = jnp.dot(k, qt, preferred_element_type=jnp.float32) * factor
        m1 = jnp.max(st, axis=0, keepdims=True)
        p = jnp.exp(st - m1)
        l1 = jnp.sum(p, axis=0, keepdims=True)
        ot = jnp.dot(vt, p.astype(jnp.bfloat16), preferred_element_type=jnp.float32)
        return m1, l1, ot

    def merge(first, ms, ls, accs, j, m1, l1, o1, mask=None):
        def put(ref, value):
            if mask is None:
                ref[j] = value
            else:
                ref[j] = jnp.where(mask, value, ref[j])

        if first:
            put(ms, m1)
            put(ls, l1)
            put(accs, o1)
        else:
            m0 = ms[j]
            mn = jnp.maximum(m0, m1)
            a = jnp.exp(m0 - mn)
            b = jnp.exp(m1 - mn)
            put(ms, mn)
            put(ls, ls[j] * a + l1 * b)
            put(accs, accs[j] * a + o1 * b)

    def tile_step(load, first):
        def one_head(h, carry):
            kcol = pl.multiple_of(h * DH, DH)
            vcol = pl.multiple_of(width_k + h * DH, DH)
            k = load(pl.ds(kcol, DH))
            vt = load(pl.ds(vcol, DH)).astype(jnp.float32).T.astype(jnp.bfloat16)
            for g in range(group // PACK):
                j = h * (group // PACK) + g
                merge(first, m_ref, l_ref, acc_ref, j, *scored(k, vt, q_ref[j]))
            merge(first, m0_ref, l0_ref, acc0_ref, 0, *scored(k, vt, q0t), mask=column_head == h)
            return carry

        lax.fori_loop(0, heads_kv, one_head, 0)

    tile_step(loaders[0], True)
    for t in range(1, tiles):

        @pl.when(meta_ref[t] > 0)
        def _(load=loaders[t]):
            tile_step(load, False)

    def finish(j, carry):
        normed = (acc_ref[j] / l_ref[j]).T.astype(out_ref.dtype)
        for s in range(PACK):
            col = pl.multiple_of((PACK * j + s) * DH, DH)
            out_ref[:, pl.ds(col, DH)] = normed[s * rows : (s + 1) * rows]
        return carry

    lax.fori_loop(0, heads // PACK, finish, 0)
    out0_ref[...] = acc0_ref[0] / l0_ref[0]


def attend(meta, q_heads, partner_stack, pieces):
    heads, _, rows = q_heads.shape
    heads, rows = PACK * heads, rows // PACK
    return pl.pallas_call(
        attention_kernel,
        out_shape=(
            jax.ShapeDtypeStruct((rows, heads * DH), jnp.bfloat16),
            jax.ShapeDtypeStruct((DH, DH), jnp.float32),
        ),
        in_specs=[pl.BlockSpec(memory_space=pltpu.SMEM)]
        + [pl.BlockSpec(memory_space=pltpu.VMEM)] * (2 + len(pieces)),
        out_specs=(pl.BlockSpec(memory_space=pltpu.VMEM), pl.BlockSpec(memory_space=pltpu.VMEM)),
        scratch_shapes=[
            pltpu.VMEM((heads // PACK, 1, PACK * rows), jnp.float32),
            pltpu.VMEM((heads // PACK, 1, PACK * rows), jnp.float32),
            pltpu.VMEM((heads // PACK, DH, PACK * rows), jnp.float32),
            pltpu.VMEM((1, 1, DH), jnp.float32),
            pltpu.VMEM((1, 1, DH), jnp.float32),
            pltpu.VMEM((1, DH, DH), jnp.float32),
        ],
        compiler_params=pltpu.CompilerParams(vmem_limit_bytes=56 * 1024 * 1024),
    )(meta, q_heads, partner_stack, *pieces)


def shards(queries, keys, values, lengths, class_weight):
    devices = lax.axis_size("seq")
    myself = lax.axis_index("seq")
    row_count = queries.shape[0]
    width_q = queries.shape[1]
    width_k = keys.shape[1]
    heads = width_q // DH
    heads_kv = width_k // DH
    group = heads // heads_kv
    arrived = lax.all_to_all(
        jnp.concatenate(
            [
                queries.reshape(devices, heads, DH),
                keys.reshape(devices, heads_kv, DH),
                values.reshape(devices, heads_kv, DH),
            ],
            axis=1,
        ),
        "seq",
        split_axis=0,
        concat_axis=0,
        tiled=True,
    )
    owner_doc, first_block = block_docs(lengths, devices)
    my_doc = owner_doc[myself]
    partner = myself + 1 - 2 * (myself % 2)
    hops = MAXB // 2
    offsets = [0]
    for hop in range(1, hops):
        offsets += [-2 * hop, 2 * hop]
    offsets = jnp.array(offsets + [0], jnp.int32)
    last = jnp.array([0] * (2 * hops - 1) + [2 * hops], jnp.int32)
    blocks = jnp.concatenate(
        [myself + offsets + last * (1 - 2 * (myself % 2)), partner + offsets + last * (1 - 2 * (partner % 2))]
    )
    inside = (blocks >= 0) & (blocks < devices)
    docs = jnp.take(owner_doc, jnp.clip(blocks, 0, devices - 1))
    flags = (inside & (docs == my_doc)).astype(jnp.int32).at[0].set(1)
    pick = jnp.argmax(blocks == first_block[myself]).astype(jnp.int32)
    meta = jnp.concatenate([flags, pick[None]])
    q_heads = (
        arrived[:, :heads]
        .reshape(row_count, heads // PACK, PACK, DH)
        .transpose(1, 3, 2, 0)
        .reshape(heads // PACK, DH, PACK * row_count)
    )
    own_q0t = jnp.pad(arrived[0, :heads].T, ((0, 0), (0, DH - heads)))
    kv = jnp.concatenate([arrived[:, heads:].reshape(row_count, 2 * width_k), own_q0t], axis=1)
    kv, meta = lax.optimization_barrier((kv, meta))
    pieces = [kv]
    right = kv
    left = kv
    for hop in range(1, hops):
        right = shifted(right, "seq", 2)
        left = shifted(left, "seq", -2)
        pieces += [right, left]
    onward = jnp.where(myself % 2 == 1, right, left)
    route = [(i, i + 2) for i in range(1, devices - 2, 2)] + [(i, i - 2) for i in range(2, devices, 2)]
    pieces.append(lax.ppermute(onward, "seq", route))
    partner_stack = lax.ppermute(
        jnp.stack(pieces), "seq", [(i, i + 1 - 2 * (i % 2)) for i in range(devices)]
    )
    attended, start_out = attend(meta, q_heads, partner_stack, pieces)
    start_row = start_out[:, :heads].T.reshape(1, width_q).astype(jnp.bfloat16)
    doc_logits = jnp.dot(start_row, class_weight, preferred_element_type=jnp.float32)
    return (attended, doc_logits)


def solution(mesh):
    return jax.shard_map(
        shards,
        mesh=mesh,
        in_specs=(P("seq", None), P("seq", None), P("seq", None), P(), P()),
        out_specs=(P("seq", None), P("seq", None)),
        check_vma=False,
    )
```

```python
import jax
import jax.numpy as jnp
from jax import lax
from jax.sharding import PartitionSpec as P
from jax.experimental import pallas as pl
from jax.experimental.pallas import tpu as pltpu

DH = 128
BLK = 128
MAXB = 8


def shifted(block, axis, distance):
    count = lax.axis_size(axis)
    if distance > 0:
        route = [(i - distance, i) for i in range(distance, count)]
    else:
        route = [(i - distance, i) for i in range(0, count + distance)]
    return lax.ppermute(block, axis, route)


def block_docs(lengths, block_count):
    doc_ends = jnp.cumsum(lengths, dtype=jnp.int32)
    doc_firsts = doc_ends - lengths
    blocks = jnp.arange(block_count, dtype=jnp.int32)
    owner_doc = jnp.sum((doc_ends[None, :] <= blocks[:, None]).astype(jnp.int32), axis=1)
    matches = owner_doc[:, None] == jnp.arange(lengths.shape[0], dtype=jnp.int32)[None, :]
    first_block = jnp.sum(jnp.where(matches, doc_firsts[None, :], 0), axis=1)
    return (owner_doc, first_block)


def attention_kernel(meta_ref, q_ref, stack_ref, *refs):
    own = len(refs) - 8
    out_ref, out0_ref, m_ref, l_ref, acc_ref, m0_ref, l0_ref, acc0_ref = refs[own:]
    rows = q_ref.shape[2] // 2
    loaders = [lambda cols, r=r: r[:, cols] for r in refs[:own]]
    loaders += [lambda cols, i=i: stack_ref[i, :, cols] for i in range(stack_ref.shape[0])]
    tiles = len(loaders)
    heads = 2 * q_ref.shape[0]
    width_k = (stack_ref.shape[2] - DH) // 2
    heads_kv = width_k // DH
    group = heads // heads_kv
    factor = DH ** (-0.5)
    q0s_ref = out0_ref

    for t in range(tiles):

        @pl.when(meta_ref[tiles] == t)
        def _(load=loaders[t]):
            q0s_ref[...] = load(pl.ds(2 * width_k, DH)).astype(jnp.float32)

    q0t = q0s_ref[...].astype(jnp.bfloat16)
    column_head = lax.broadcasted_iota(jnp.int32, (1, DH), 1) // group

    def scored(k, vt, qt):
        st = jnp.dot(k, qt, preferred_element_type=jnp.float32) * factor
        m1 = jnp.max(st, axis=0, keepdims=True)
        p = jnp.exp(st - m1)
        l1 = jnp.sum(p, axis=0, keepdims=True)
        ot = jnp.dot(vt, p.astype(jnp.bfloat16), preferred_element_type=jnp.float32)
        return m1, l1, ot

    def merge(first, ms, ls, accs, j, m1, l1, o1, mask=None):
        def put(ref, value):
            if mask is None:
                ref[j] = value
            else:
                ref[j] = jnp.where(mask, value, ref[j])

        if first:
            put(ms, m1)
            put(ls, l1)
            put(accs, o1)
        else:
            m0 = ms[j]
            mn = jnp.maximum(m0, m1)
            a = jnp.exp(m0 - mn)
            b = jnp.exp(m1 - mn)
            put(ms, mn)
            put(ls, ls[j] * a + l1 * b)
            put(accs, accs[j] * a + o1 * b)

    def tile_step(load, first):
        def one_head(h, carry):
            kcol = pl.multiple_of(h * DH, DH)
            vcol = pl.multiple_of(width_k + h * DH, DH)
            k = load(pl.ds(kcol, DH))
            vt = load(pl.ds(vcol, DH)).astype(jnp.float32).T.astype(jnp.bfloat16)
            for g in range(group // 2):
                j = h * (group // 2) + g
                merge(first, m_ref, l_ref, acc_ref, j, *scored(k, vt, q_ref[j]))
            merge(first, m0_ref, l0_ref, acc0_ref, 0, *scored(k, vt, q0t), mask=column_head == h)
            return carry

        lax.fori_loop(0, heads_kv, one_head, 0)

    tile_step(loaders[0], True)
    for t in range(1, tiles):

        @pl.when(meta_ref[t] > 0)
        def _(load=loaders[t]):
            tile_step(load, False)

    def finish(j, carry):
        normed = (acc_ref[j] * (1.0 / l_ref[j])).T.astype(out_ref.dtype)
        out_ref[:, pl.ds(pl.multiple_of(2 * j * DH, DH), DH)] = normed[:rows]
        out_ref[:, pl.ds(pl.multiple_of((2 * j + 1) * DH, DH), DH)] = normed[rows:]
        return carry

    lax.fori_loop(0, heads // 2, finish, 0)
    out0_ref[...] = acc0_ref[0] / l0_ref[0]


def attend(meta, q_heads, partner_stack, pieces):
    heads, _, rows = q_heads.shape
    heads, rows = 2 * heads, rows // 2
    return pl.pallas_call(
        attention_kernel,
        out_shape=(
            jax.ShapeDtypeStruct((rows, heads * DH), jnp.bfloat16),
            jax.ShapeDtypeStruct((DH, DH), jnp.float32),
        ),
        in_specs=[pl.BlockSpec(memory_space=pltpu.SMEM)]
        + [pl.BlockSpec(memory_space=pltpu.VMEM)] * (2 + len(pieces)),
        out_specs=(pl.BlockSpec(memory_space=pltpu.VMEM), pl.BlockSpec(memory_space=pltpu.VMEM)),
        scratch_shapes=[
            pltpu.VMEM((heads // 2, 1, 2 * rows), jnp.float32),
            pltpu.VMEM((heads // 2, 1, 2 * rows), jnp.float32),
            pltpu.VMEM((heads // 2, DH, 2 * rows), jnp.float32),
            pltpu.VMEM((1, 1, DH), jnp.float32),
            pltpu.VMEM((1, 1, DH), jnp.float32),
            pltpu.VMEM((1, DH, DH), jnp.float32),
        ],
        compiler_params=pltpu.CompilerParams(vmem_limit_bytes=56 * 1024 * 1024),
    )(meta, q_heads, partner_stack, *pieces)


def shards(queries, keys, values, lengths, class_weight):
    devices = lax.axis_size("seq")
    myself = lax.axis_index("seq")
    row_count = queries.shape[0]
    width_q = queries.shape[1]
    width_k = keys.shape[1]
    heads = width_q // DH
    heads_kv = width_k // DH
    group = heads // heads_kv
    arrived = lax.all_to_all(
        jnp.concatenate(
            [
                queries.reshape(devices, heads, DH),
                keys.reshape(devices, heads_kv, DH),
                values.reshape(devices, heads_kv, DH),
            ],
            axis=1,
        ),
        "seq",
        split_axis=0,
        concat_axis=0,
        tiled=True,
    )
    owner_doc, first_block = block_docs(lengths, devices)
    my_doc = owner_doc[myself]
    partner = myself + 1 - 2 * (myself % 2)
    hops = MAXB // 2
    offsets = [0]
    for hop in range(1, hops):
        offsets += [-2 * hop, 2 * hop]
    offsets = jnp.array(offsets + [0], jnp.int32)
    last = jnp.array([0] * (2 * hops - 1) + [2 * hops], jnp.int32)
    blocks = jnp.concatenate(
        [myself + offsets + last * (1 - 2 * (myself % 2)), partner + offsets + last * (1 - 2 * (partner % 2))]
    )
    inside = (blocks >= 0) & (blocks < devices)
    docs = jnp.take(owner_doc, jnp.clip(blocks, 0, devices - 1))
    flags = (inside & (docs == my_doc)).astype(jnp.int32).at[0].set(1)
    pick = jnp.argmax(blocks == first_block[myself]).astype(jnp.int32)
    meta = jnp.concatenate([flags, pick[None]])
    q_heads = (
        arrived[:, :heads]
        .reshape(row_count, heads // 2, 2, DH)
        .transpose(1, 3, 2, 0)
        .reshape(heads // 2, DH, 2 * row_count)
    )
    own_q0t = jnp.pad(arrived[0, :heads].T, ((0, 0), (0, DH - heads)))
    kv = jnp.concatenate([arrived[:, heads:].reshape(row_count, 2 * width_k), own_q0t], axis=1)
    kv, meta = lax.optimization_barrier((kv, meta))
    pieces = [kv]
    right = kv
    left = kv
    for hop in range(1, hops):
        right = shifted(right, "seq", 2)
        left = shifted(left, "seq", -2)
        pieces += [right, left]
    onward = jnp.where(myself % 2 == 1, right, left)
    route = [(i, i + 2) for i in range(1, devices - 2, 2)] + [(i, i - 2) for i in range(2, devices, 2)]
    pieces.append(lax.ppermute(onward, "seq", route))
    partner_stack = lax.ppermute(
        jnp.stack(pieces), "seq", [(i, i + 1 - 2 * (i % 2)) for i in range(devices)]
    )
    attended, start_out = attend(meta, q_heads, partner_stack, pieces)
    start_row = start_out[:, :heads].T.reshape(1, width_q).astype(jnp.bfloat16)
    doc_logits = jnp.dot(start_row, class_weight, preferred_element_type=jnp.float32)
    return (attended, doc_logits)


def solution(mesh):
    return jax.shard_map(
        shards,
        mesh=mesh,
        in_specs=(P("seq", None), P("seq", None), P("seq", None), P(), P()),
        out_specs=(P("seq", None), P("seq", None)),
        check_vma=False,
    )
```

```python
import jax
import jax.numpy as jnp
from jax import lax
from jax.sharding import PartitionSpec as P
from jax.experimental import pallas as pl
from jax.experimental.pallas import tpu as pltpu

DH = 128
BLK = 128
MAXB = 8


def shifted(block, axis, distance):
    count = lax.axis_size(axis)
    if distance > 0:
        route = [(i - distance, i) for i in range(distance, count)]
    else:
        route = [(i - distance, i) for i in range(0, count + distance)]
    return lax.ppermute(block, axis, route)


def block_docs(lengths, block_count):
    doc_ends = jnp.cumsum(lengths, dtype=jnp.int32)
    doc_firsts = doc_ends - lengths
    blocks = jnp.arange(block_count, dtype=jnp.int32)
    owner_doc = jnp.sum((doc_ends[None, :] <= blocks[:, None]).astype(jnp.int32), axis=1)
    matches = owner_doc[:, None] == jnp.arange(lengths.shape[0], dtype=jnp.int32)[None, :]
    first_block = jnp.sum(jnp.where(matches, doc_firsts[None, :], 0), axis=1)
    return (owner_doc, first_block)


def attention_kernel(meta_ref, q_ref, stack_ref, *refs):
    own = len(refs) - 8
    out_ref, out0_ref, m_ref, l_ref, acc_ref, m0_ref, l0_ref, acc0_ref = refs[own:]
    rows = q_ref.shape[2] // 2
    loaders = [lambda cols, r=r: r[:, cols] for r in refs[:own]]
    loaders += [lambda cols, i=i: stack_ref[i, :, cols] for i in range(stack_ref.shape[0])]
    tiles = len(loaders)
    heads = 2 * q_ref.shape[0]
    width_k = (stack_ref.shape[2] - DH) // 2
    heads_kv = width_k // DH
    group = heads // heads_kv
    factor = DH ** (-0.5)
    q0s_ref = out0_ref

    for t in range(tiles):

        @pl.when(meta_ref[tiles] == t)
        def _(load=loaders[t]):
            q0s_ref[...] = load(pl.ds(2 * width_k, DH)).astype(jnp.float32)

    q0t = q0s_ref[...].astype(jnp.bfloat16)
    column_head = lax.broadcasted_iota(jnp.int32, (1, DH), 1) // group

    def scored(k, vt, qt):
        st = jnp.dot(k, qt, preferred_element_type=jnp.float32) * factor
        m1 = jnp.max(st, axis=0, keepdims=True)
        p = jnp.exp(st - m1)
        l1 = jnp.sum(p, axis=0, keepdims=True)
        ot = jnp.dot(vt, p.astype(jnp.bfloat16), preferred_element_type=jnp.float32)
        return m1, l1, ot

    def merge(first, ms, ls, accs, j, m1, l1, o1, mask=None):
        def put(ref, value):
            if mask is None:
                ref[j] = value
            else:
                ref[j] = jnp.where(mask, value, ref[j])

        if first:
            put(ms, m1)
            put(ls, l1)
            put(accs, o1)
        else:
            m0 = ms[j]
            mn = jnp.maximum(m0, m1)
            a = jnp.exp(m0 - mn)
            b = jnp.exp(m1 - mn)
            put(ms, mn)
            put(ls, ls[j] * a + l1 * b)
            put(accs, accs[j] * a + o1 * b)

    def tile_step(load, first):
        def one_head(h, carry):
            kcol = pl.multiple_of(h * DH, DH)
            vcol = pl.multiple_of(width_k + h * DH, DH)
            k = load(pl.ds(kcol, DH))
            vt = load(pl.ds(vcol, DH)).astype(jnp.float32).T.astype(jnp.bfloat16)
            for g in range(group // 2):
                j = h * (group // 2) + g
                merge(first, m_ref, l_ref, acc_ref, j, *scored(k, vt, q_ref[j]))
            merge(first, m0_ref, l0_ref, acc0_ref, 0, *scored(k, vt, q0t), mask=column_head == h)
            return carry

        lax.fori_loop(0, heads_kv, one_head, 0, unroll=2)

    tile_step(loaders[0], True)
    for t in range(1, tiles):

        @pl.when(meta_ref[t] > 0)
        def _(load=loaders[t]):
            tile_step(load, False)

    def finish(j, carry):
        normed = (acc_ref[j] / l_ref[j]).T.astype(out_ref.dtype)
        out_ref[:, pl.ds(pl.multiple_of(2 * j * DH, DH), DH)] = normed[:rows]
        out_ref[:, pl.ds(pl.multiple_of((2 * j + 1) * DH, DH), DH)] = normed[rows:]
        return carry

    lax.fori_loop(0, heads // 2, finish, 0)
    out0_ref[...] = acc0_ref[0] / l0_ref[0]


def attend(meta, q_heads, partner_stack, pieces):
    heads, _, rows = q_heads.shape
    heads, rows = 2 * heads, rows // 2
    return pl.pallas_call(
        attention_kernel,
        out_shape=(
            jax.ShapeDtypeStruct((rows, heads * DH), jnp.bfloat16),
            jax.ShapeDtypeStruct((DH, DH), jnp.float32),
        ),
        in_specs=[pl.BlockSpec(memory_space=pltpu.SMEM)]
        + [pl.BlockSpec(memory_space=pltpu.VMEM)] * (2 + len(pieces)),
        out_specs=(pl.BlockSpec(memory_space=pltpu.VMEM), pl.BlockSpec(memory_space=pltpu.VMEM)),
        scratch_shapes=[
            pltpu.VMEM((heads // 2, 1, 2 * rows), jnp.float32),
            pltpu.VMEM((heads // 2, 1, 2 * rows), jnp.float32),
            pltpu.VMEM((heads // 2, DH, 2 * rows), jnp.float32),
            pltpu.VMEM((1, 1, DH), jnp.float32),
            pltpu.VMEM((1, 1, DH), jnp.float32),
            pltpu.VMEM((1, DH, DH), jnp.float32),
        ],
        compiler_params=pltpu.CompilerParams(vmem_limit_bytes=56 * 1024 * 1024),
    )(meta, q_heads, partner_stack, *pieces)


def shards(queries, keys, values, lengths, class_weight):
    devices = lax.axis_size("seq")
    myself = lax.axis_index("seq")
    row_count = queries.shape[0]
    width_q = queries.shape[1]
    width_k = keys.shape[1]
    heads = width_q // DH
    heads_kv = width_k // DH
    group = heads // heads_kv
    arrived = lax.all_to_all(
        jnp.concatenate(
            [
                queries.reshape(devices, heads, DH),
                keys.reshape(devices, heads_kv, DH),
                values.reshape(devices, heads_kv, DH),
            ],
            axis=1,
        ),
        "seq",
        split_axis=0,
        concat_axis=0,
        tiled=True,
    )
    owner_doc, first_block = block_docs(lengths, devices)
    my_doc = owner_doc[myself]
    partner = myself + 1 - 2 * (myself % 2)
    hops = MAXB // 2
    offsets = [0]
    for hop in range(1, hops):
        offsets += [-2 * hop, 2 * hop]
    offsets = jnp.array(offsets + [0], jnp.int32)
    last = jnp.array([0] * (2 * hops - 1) + [2 * hops], jnp.int32)
    blocks = jnp.concatenate(
        [myself + offsets + last * (1 - 2 * (myself % 2)), partner + offsets + last * (1 - 2 * (partner % 2))]
    )
    inside = (blocks >= 0) & (blocks < devices)
    docs = jnp.take(owner_doc, jnp.clip(blocks, 0, devices - 1))
    flags = (inside & (docs == my_doc)).astype(jnp.int32).at[0].set(1)
    pick = jnp.argmax(blocks == first_block[myself]).astype(jnp.int32)
    meta = jnp.concatenate([flags, pick[None]])
    q_heads = (
        arrived[:, :heads]
        .reshape(row_count, heads // 2, 2, DH)
        .transpose(1, 3, 2, 0)
        .reshape(heads // 2, DH, 2 * row_count)
    )
    own_q0t = jnp.pad(arrived[0, :heads].T, ((0, 0), (0, DH - heads)))
    kv = jnp.concatenate([arrived[:, heads:].reshape(row_count, 2 * width_k), own_q0t], axis=1)
    kv, meta = lax.optimization_barrier((kv, meta))
    pieces = [kv]
    right = kv
    left = kv
    for hop in range(1, hops):
        right = shifted(right, "seq", 2)
        left = shifted(left, "seq", -2)
        pieces += [right, left]
    onward = jnp.where(myself % 2 == 1, right, left)
    route = [(i, i + 2) for i in range(1, devices - 2, 2)] + [(i, i - 2) for i in range(2, devices, 2)]
    pieces.append(lax.ppermute(onward, "seq", route))
    partner_stack = lax.ppermute(
        jnp.stack(pieces), "seq", [(i, i + 1 - 2 * (i % 2)) for i in range(devices)]
    )
    attended, start_out = attend(meta, q_heads, partner_stack, pieces)
    start_row = start_out[:, :heads].T.reshape(1, width_q).astype(jnp.bfloat16)
    doc_logits = jnp.dot(start_row, class_weight, preferred_element_type=jnp.float32)
    return (attended, doc_logits)


def solution(mesh):
    return jax.shard_map(
        shards,
        mesh=mesh,
        in_specs=(P("seq", None), P("seq", None), P("seq", None), P(), P()),
        out_specs=(P("seq", None), P("seq", None)),
        check_vma=False,
    )
```

```python
import jax
import jax.numpy as jnp
from jax import lax
from jax.sharding import PartitionSpec as P
from jax.experimental import pallas as pl
from jax.experimental.pallas import tpu as pltpu

DH = 128
BLK = 128
MAXB = 8


def shifted(block, axis, distance):
    count = lax.axis_size(axis)
    if distance > 0:
        route = [(i - distance, i) for i in range(distance, count)]
    else:
        route = [(i - distance, i) for i in range(0, count + distance)]
    return lax.ppermute(block, axis, route)


def block_docs(lengths, block_count):
    doc_ends = jnp.cumsum(lengths, dtype=jnp.int32)
    doc_firsts = doc_ends - lengths
    blocks = jnp.arange(block_count, dtype=jnp.int32)
    owner_doc = jnp.sum((doc_ends[None, :] <= blocks[:, None]).astype(jnp.int32), axis=1)
    matches = owner_doc[:, None] == jnp.arange(lengths.shape[0], dtype=jnp.int32)[None, :]
    first_block = jnp.sum(jnp.where(matches, doc_firsts[None, :], 0), axis=1)
    return (owner_doc, first_block)


def attention_kernel(meta_ref, q_ref, stack_ref, *refs):
    own = len(refs) - 8
    out_ref, out0_ref, m_ref, l_ref, acc_ref, m0_ref, l0_ref, acc0_ref = refs[own:]
    rows = q_ref.shape[2] // 2
    loaders = [lambda cols, r=r: r[:, cols] for r in refs[:own]]
    loaders += [lambda cols, i=i: stack_ref[i, :, cols] for i in range(stack_ref.shape[0])]
    tiles = len(loaders)
    heads = 2 * q_ref.shape[0]
    width_k = (stack_ref.shape[2] - DH) // 2
    heads_kv = width_k // DH
    group = heads // heads_kv
    factor = DH ** (-0.5)
    q0s_ref = out0_ref

    for t in range(tiles):

        @pl.when(meta_ref[tiles] == t)
        def _(load=loaders[t]):
            q0s_ref[...] = load(pl.ds(2 * width_k, DH)).astype(jnp.float32)

    q0t = q0s_ref[...].astype(jnp.bfloat16)
    column_head = lax.broadcasted_iota(jnp.int32, (1, DH), 1) // group

    def scored(k, vt, qt):
        st = jnp.dot(k, qt, preferred_element_type=jnp.float32) * factor
        m1 = jnp.max(st, axis=0, keepdims=True)
        p = jnp.exp(st - m1)
        l1 = jnp.sum(p, axis=0, keepdims=True)
        ot = jnp.dot(vt, p.astype(jnp.bfloat16), preferred_element_type=jnp.float32)
        return m1, l1, ot

    def merge(first, ms, ls, accs, j, m1, l1, o1, mask=None):
        def put(ref, value):
            if mask is None:
                ref[j] = value
            else:
                ref[j] = jnp.where(mask, value, ref[j])

        if first:
            put(ms, m1)
            put(ls, l1)
            put(accs, o1)
        else:
            m0 = ms[j]
            mn = jnp.maximum(m0, m1)
            a = jnp.exp(m0 - mn)
            b = jnp.exp(m1 - mn)
            put(ms, mn)
            put(ls, ls[j] * a + l1 * b)
            put(accs, accs[j] * a + o1 * b)

    def tile_step(load, first):
        def one_head(h, carry):
            kcol = pl.multiple_of(h * DH, DH)
            vcol = pl.multiple_of(width_k + h * DH, DH)
            k = load(pl.ds(kcol, DH))
            vt = load(pl.ds(vcol, DH)).astype(jnp.float32).T.astype(jnp.bfloat16)
            for g in range(group // 2):
                j = h * (group // 2) + g
                merge(first, m_ref, l_ref, acc_ref, j, *scored(k, vt, q_ref[j]))
            merge(first, m0_ref, l0_ref, acc0_ref, 0, *scored(k, vt, q0t), mask=column_head == h)
            return carry

        lax.fori_loop(0, heads_kv, one_head, 0, unroll=2)

    tile_step(loaders[0], True)
    for t in range(1, tiles):

        @pl.when(meta_ref[t] > 0)
        def _(load=loaders[t]):
            tile_step(load, False)

    def finish(j, carry):
        normed = (acc_ref[j] / l_ref[j]).T.astype(out_ref.dtype)
        out_ref[:, pl.ds(pl.multiple_of(2 * j * DH, DH), DH)] = normed[:rows]
        out_ref[:, pl.ds(pl.multiple_of((2 * j + 1) * DH, DH), DH)] = normed[rows:]
        return carry

    lax.fori_loop(0, heads // 2, finish, 0, unroll=2)
    out0_ref[...] = acc0_ref[0] / l0_ref[0]


def attend(meta, q_heads, partner_stack, pieces):
    heads, _, rows = q_heads.shape
    heads, rows = 2 * heads, rows // 2
    return pl.pallas_call(
        attention_kernel,
        out_shape=(
            jax.ShapeDtypeStruct((rows, heads * DH), jnp.bfloat16),
            jax.ShapeDtypeStruct((DH, DH), jnp.float32),
        ),
        in_specs=[pl.BlockSpec(memory_space=pltpu.SMEM)]
        + [pl.BlockSpec(memory_space=pltpu.VMEM)] * (2 + len(pieces)),
        out_specs=(pl.BlockSpec(memory_space=pltpu.VMEM), pl.BlockSpec(memory_space=pltpu.VMEM)),
        scratch_shapes=[
            pltpu.VMEM((heads // 2, 1, 2 * rows), jnp.float32),
            pltpu.VMEM((heads // 2, 1, 2 * rows), jnp.float32),
            pltpu.VMEM((heads // 2, DH, 2 * rows), jnp.float32),
            pltpu.VMEM((1, 1, DH), jnp.float32),
            pltpu.VMEM((1, 1, DH), jnp.float32),
            pltpu.VMEM((1, DH, DH), jnp.float32),
        ],
        compiler_params=pltpu.CompilerParams(vmem_limit_bytes=56 * 1024 * 1024),
    )(meta, q_heads, partner_stack, *pieces)


def shards(queries, keys, values, lengths, class_weight):
    devices = lax.axis_size("seq")
    myself = lax.axis_index("seq")
    row_count = queries.shape[0]
    width_q = queries.shape[1]
    width_k = keys.shape[1]
    heads = width_q // DH
    heads_kv = width_k // DH
    group = heads // heads_kv
    arrived = lax.all_to_all(
        jnp.concatenate(
            [
                queries.reshape(devices, heads, DH),
                keys.reshape(devices, heads_kv, DH),
                values.reshape(devices, heads_kv, DH),
            ],
            axis=1,
        ),
        "seq",
        split_axis=0,
        concat_axis=0,
        tiled=True,
    )
    owner_doc, first_block = block_docs(lengths, devices)
    my_doc = owner_doc[myself]
    partner = myself + 1 - 2 * (myself % 2)
    hops = MAXB // 2
    offsets = [0]
    for hop in range(1, hops):
        offsets += [-2 * hop, 2 * hop]
    offsets = jnp.array(offsets + [0], jnp.int32)
    last = jnp.array([0] * (2 * hops - 1) + [2 * hops], jnp.int32)
    blocks = jnp.concatenate(
        [myself + offsets + last * (1 - 2 * (myself % 2)), partner + offsets + last * (1 - 2 * (partner % 2))]
    )
    inside = (blocks >= 0) & (blocks < devices)
    docs = jnp.take(owner_doc, jnp.clip(blocks, 0, devices - 1))
    flags = (inside & (docs == my_doc)).astype(jnp.int32).at[0].set(1)
    pick = jnp.argmax(blocks == first_block[myself]).astype(jnp.int32)
    meta = jnp.concatenate([flags, pick[None]])
    q_heads = (
        arrived[:, :heads]
        .reshape(row_count, heads // 2, 2, DH)
        .transpose(1, 3, 2, 0)
        .reshape(heads // 2, DH, 2 * row_count)
    )
    own_q0t = jnp.pad(arrived[0, :heads].T, ((0, 0), (0, DH - heads)))
    kv = jnp.concatenate([arrived[:, heads:].reshape(row_count, 2 * width_k), own_q0t], axis=1)
    kv, meta = lax.optimization_barrier((kv, meta))
    pieces = [kv]
    right = kv
    left = kv
    for hop in range(1, hops):
        right = shifted(right, "seq", 2)
        left = shifted(left, "seq", -2)
        pieces += [right, left]
    onward = jnp.where(myself % 2 == 1, right, left)
    route = [(i, i + 2) for i in range(1, devices - 2, 2)] + [(i, i - 2) for i in range(2, devices, 2)]
    pieces.append(lax.ppermute(onward, "seq", route))
    partner_stack = lax.ppermute(
        jnp.stack(pieces), "seq", [(i, i + 1 - 2 * (i % 2)) for i in range(devices)]
    )
    attended, start_out = attend(meta, q_heads, partner_stack, pieces)
    start_row = start_out[:, :heads].T.reshape(1, width_q).astype(jnp.bfloat16)
    doc_logits = jnp.dot(start_row, class_weight, preferred_element_type=jnp.float32)
    return (attended, doc_logits)


def solution(mesh):
    return jax.shard_map(
        shards,
        mesh=mesh,
        in_specs=(P("seq", None), P("seq", None), P("seq", None), P(), P()),
        out_specs=(P("seq", None), P("seq", None)),
        check_vma=False,
    )
```
